32 devices in a mesh: survey: 2 (over x), dom: 16 (over z, y, core).
Axes of the slice: x: 2, y: 2, z: 4, core: 2. Of those that a mesh axis runs over, the one named last changes fastest.
Arguments:
- older_fields: float32 [2, 256, 128, 128], P(None, 'survey', 'dom'), parts along dimension 1, may hold values from -6 to 6
- fields_now: float32 [2, 256, 128, 128], P(None, 'survey', 'dom'), parts along dimension 1, may hold values from -6 to 6
- velocity: float32 [128, 256, 128], P('dom', 'survey'), parts along dimension 1, may hold values from 1.5 to 4.5
- aperture: int32 [32], P('survey'), parts along dimension 0, may hold values from 0 to 15, as said below
- source_pos: int32 [3, 16], P(None, 'survey'), parts along dimension 1, may hold values from 0 to 127, as said below
- wavelet: float32 [20, 16], P(None, 'survey'), parts along dimension 1, may hold values from -16 to 16
- receiver_pos: int32 [3, 16384], P(None, 'survey'), parts along dimension 1, may hold values from 0 to 127, as said below
- traces: float32 [20, 16384], P(None, 'survey'), parts along dimension 1, may hold values from -16 to 16
Outputs:
- older_out: float32 [2, 256, 128, 128], P(None, 'survey', 'dom'), parts along dimension 1
- fields_out: float32 [2, 256, 128, 128], P(None, 'survey', 'dom'), parts along dimension 1
- image_model: float32 [128, 256, 128], P('dom', 'survey'), parts along dimension 1
The draws below stay inside these ranges and needn't reach their ends.
There are 2 independent parts, one for each index of `survey`. The reference program is written for one: setup_inputs(seed, part) draws one part's arguments, and reference() takes and returns one part's arrays. A program takes and returns all parts, laid end to end along the dimension named above; each array names one. Nothing has to cross between parts.
Inputs may be any that keep to these rules, and one draw needn't show every extreme that they name: aperture[j] = min(max(j + s, 0), 15) for one shift s with |s| <= 4. `source_pos`: row 0 holds x below 128, row 1 y below 128, row 2 depth below 4. `receiver_pos`: row 0 holds x below 128, row 1 y below 128, row 2 depth below 4.
All inputs are finite; a program needn't handle non-finite values.
Results may differ from the reference program's by a relative error of at most 0.0003.
Values sent between devices are 32-bit elements; how exact they have to be, the bound alone decides.
No kernel may reach another device: no remote copies, remote signals or barrier semaphores. Data moves between devices by JAX's collectives and lax.ppermute only.
A program may use at most 64 MiB of HBM per device.

```python
import jax
import jax.numpy as jnp
from jax import lax

CX = 8
NY = 128
NZ = 128
STEPS = 20
NSRC = 8
NREC = 8192
SLABS = 16
NX = 128


def draw_aperture(key, part):
    shift_by = jax.random.randint(jax.random.fold_in(key, 11), (), -(SLABS // 4), SLABS // 4 + 1)
    return jnp.clip(jnp.arange(SLABS, dtype=jnp.int32) + shift_by, 0, SLABS - 1).astype(jnp.int32)


def place_cells(key, count):
    along_x = jax.random.randint(jax.random.fold_in(key, 1), (count,), 0, NX)
    along_y = jax.random.randint(jax.random.fold_in(key, 2), (count,), 0, NY)
    depth_cell = jax.random.randint(jax.random.fold_in(key, 3), (count,), 0, 4)
    along_x = along_x.at[0].set(NX - 1)
    along_y = along_y.at[1].set(NY - 1)
    return jnp.stack([along_x, along_y, depth_cell]).astype(jnp.int32)


def draw_source_pos(key, part):
    return place_cells(jax.random.fold_in(key, 101), NSRC)


def draw_receiver_pos(key, part):
    return place_cells(jax.random.fold_in(key, 202), NREC)


def shard_levels(own_key, extent, split, smallest, largest):
    level, own = 1.0, jax.random.fold_in(own_key, 6)
    for dim, blocks in split:
        steps = jnp.exp(jax.random.uniform(jax.random.fold_in(own, dim), (blocks,), jnp.float32, smallest / len(split), largest / len(split)))
        level = level * jnp.repeat(steps, extent[dim] // blocks).reshape([-1 if axis == dim else 1 for axis in range(len(extent))])
    return level


def gaussian(key, dims, deviation, limit, split=(), held_as=jnp.bfloat16):
    entries = jax.random.normal(key, dims, jnp.float32) * deviation
    if len(split) > 0:
        entries = shard_levels(key, dims, split, -0.22, 0.18) * entries
    return jnp.clip(entries, min=-limit, max=limit).astype(held_as)


def setup_inputs(seed: int = 0, part: int = 0) -> dict:
    key_of = jax.random.split(jax.random.key(seed), 9)
    own_keys = jax.random.split(jax.random.fold_in(key_of[8], part), 9)
    return {
        "older_fields": gaussian(own_keys[0], (2, NY, NX, NZ), 1.0, 6.0, ((2, 16),), jnp.float32),
        "fields_now": gaussian(own_keys[1], (2, NY, NX, NZ), 1.0, 6.0, ((2, 16),), jnp.float32),
        "velocity": jnp.clip(1.5 + 3.0 * jax.random.uniform(own_keys[2], (NY, NX, NZ), jnp.float32) ** shard_levels(own_keys[2], (NY, NX, NZ), ((0, 16),), -0.2, 0.2), 1.5, 4.5),
        "aperture": draw_aperture(jax.random.fold_in(jax.random.fold_in(key_of[8], part), 71), part),
        "source_pos": draw_source_pos(jax.random.fold_in(jax.random.fold_in(key_of[8], part), 71), part),
        "wavelet": gaussian(own_keys[5], (STEPS, NSRC), 4.0, 16.0, (), jnp.float32),
        "receiver_pos": draw_receiver_pos(jax.random.fold_in(jax.random.fold_in(key_of[8], part), 71), part),
        "traces": gaussian(own_keys[7], (STEPS, NREC), 4.0, 16.0, (), jnp.float32),
    }


courant = 0.09
stencil_weights = (8.0 / 5.0, -1.0 / 5.0, 8.0 / 315.0, -1.0 / 560.0)
center_weight = 3.0 * (-205.0 / 72.0)


def laplace(extended):
    cells_wide = extended.shape[2] - 8
    depth_y = extended.shape[1]
    depth_z = extended.shape[3]
    middle = extended[:, :, 4:4 + cells_wide, :]
    padded = jnp.pad(middle, ((0, 0), (4, 4), (0, 0), (4, 4)))
    summed = center_weight * middle
    for offset in range(1, 5):
        weight = stencil_weights[offset - 1]
        beside_all = extended[:, :, 4 + offset:4 + offset + cells_wide, :] + extended[:, :, 4 - offset:4 - offset + cells_wide, :]
        beside_all = beside_all + padded[:, 4 + offset:4 + offset + depth_y, :, 4:4 + depth_z] + padded[:, 4 - offset:4 - offset + depth_y, :, 4:4 + depth_z]
        beside_all = beside_all + padded[:, 4:4 + depth_y, :, 4 + offset:4 + offset + depth_z] + padded[:, 4:4 + depth_y, :, 4 - offset:4 - offset + depth_z]
        summed = summed + weight * beside_all
    return summed


def deposit(values, component, cell_rows, amounts, x_start):
    cells_wide = values.shape[2]
    local_x = cell_rows[0] - x_start
    inside = (local_x >= 0) & (local_x < cells_wide)
    local_x = jnp.where(inside, local_x, cells_wide)
    return values.at[component, cell_rows[1], local_x, cell_rows[2]].add(amounts, mode="drop")


def inject(laplacian, source_pos, receiver_pos, pulses, recorded, x_start):
    laplacian = deposit(laplacian, 0, source_pos, pulses, x_start)
    return deposit(laplacian, 1, receiver_pos, recorded, x_start)


def reference(older_fields, fields_now, velocity, aperture, source_pos, wavelet, receiver_pos, traces):
    bricks = velocity.reshape(NY, SLABS, CX, NZ)
    speed_dom = jnp.take(bricks, aperture, axis=1).reshape(NY, NX, NZ)
    scaled = courant * speed_dom
    speed_sq = scaled * scaled
    previous = older_fields
    current = fields_now
    image_acc = jnp.zeros((NY, NX, NZ), jnp.float32)
    for moment in range(STEPS):
        extended = jnp.pad(current, ((0, 0), (0, 0), (4, 4), (0, 0)))
        laplacian = inject(laplace(extended), source_pos, receiver_pos, wavelet[moment], traces[moment], 0)
        updated = 2.0 * current - previous + speed_sq[None] * laplacian
        image_acc = image_acc + updated[0] * updated[1]
        previous = current
        current = updated
    image_acc = image_acc * (1.0 / STEPS)
    one_hot = (aperture[None, :] == jnp.arange(SLABS, dtype=jnp.int32)[:, None]).astype(jnp.float32)
    blocked = image_acc.reshape(NY, SLABS, CX, NZ)
    summed = jnp.einsum("mj,yjcz->ymcz", one_hot, blocked, precision=lax.Precision.HIGHEST)
    return previous, current, summed.reshape(NY, NX, NZ)
```

```python
import functools

import jax
import jax.numpy as jnp
from jax import lax
from jax.experimental import pallas as pl
from jax.experimental.pallas import tpu as pltpu
from jax.sharding import PartitionSpec as P

courant = 0.09
stencil_weights = (8.0 / 5.0, -1.0 / 5.0, 8.0 / 315.0, -1.0 / 560.0)
center_weight = 3.0 * (-205.0 / 72.0)
HALO = 4
XOFF = 8


def with_halo(cells, axis, dim, width):
    count = lax.axis_size(axis)
    ends = count - 1
    head = lax.slice_in_dim(cells, 0, width, axis=dim)
    tail = lax.slice_in_dim(cells, cells.shape[dim] - width, cells.shape[dim], axis=dim)
    low = lax.ppermute(tail, axis, [(i, (i + 1) % count) for i in range(ends)])
    high = lax.ppermute(head, axis, [((i + 1) % count, i) for i in range(ends)])
    return low, high


def step_kernel(
    cur_ref, prev_ref, s_ref, img_ref, xlo_ref, xhi_ref, inj_ref, out_ref, imgo_ref, ext_ref
):
    comps, block_y, block_x, depth_z = cur_ref.shape
    zeros_y = jnp.zeros((comps, HALO, block_x, depth_z), jnp.float32)
    ext_ref[:, 0:HALO, XOFF : XOFF + block_x, :] = zeros_y
    ext_ref[:, HALO + block_y : 2 * HALO + block_y, XOFF : XOFF + block_x, :] = zeros_y
    ext_ref[:, HALO : HALO + block_y, XOFF - HALO : XOFF, :] = xlo_ref[...]
    ext_ref[:, HALO : HALO + block_y, XOFF : XOFF + block_x, :] = cur_ref[...]
    ext_ref[:, HALO : HALO + block_y, XOFF + block_x : XOFF + block_x + HALO, :] = xhi_ref[...]
    lane = lax.broadcasted_iota(jnp.int32, (block_x, depth_z), 1)

    def row(y, carry):
        done = []
        for c in range(comps):
            ctr = cur_ref[c, y]
            acc = center_weight * ctr
            for m in range(1, HALO + 1):
                b = ext_ref[c, HALO + y, XOFF + m : XOFF + m + block_x, :] + ext_ref[
                    c, HALO + y, XOFF - m : XOFF - m + block_x, :
                ]
                b = (
                    b
                    + ext_ref[c, HALO + y + m, XOFF : XOFF + block_x, :]
                    + ext_ref[c, HALO + y - m, XOFF : XOFF + block_x, :]
                )
                up = jnp.where(lane < depth_z - m, pltpu.roll(ctr, depth_z - m, 1), 0.0)
                down = jnp.where(lane >= m, pltpu.roll(ctr, m, 1), 0.0)
                b = b + up + down
                acc = acc + stencil_weights[m - 1] * b
            lap = acc + inj_ref[c, y]
            upd = 2.0 * ctr - prev_ref[c, y] + s_ref[y] * lap
            out_ref[c, y] = upd
            done.append(upd)
        imgo_ref[y] = img_ref[y] + done[0] * done[1]
        return carry

    lax.fori_loop(0, block_y, row, 0)


def step_call(cur, prev, s, img, xlo, xhi, inj):
    comps, block_y, block_x, depth_z = cur.shape
    vmem = pl.BlockSpec(memory_space=pltpu.VMEM)
    return pl.pallas_call(
        step_kernel,
        out_shape=(
            jax.ShapeDtypeStruct(cur.shape, jnp.float32),
            jax.ShapeDtypeStruct(img.shape, jnp.float32),
        ),
        in_specs=[vmem] * 7,
        out_specs=(vmem, vmem),
        scratch_shapes=[
            pltpu.VMEM((comps, block_y + 2 * HALO, block_x + 2 * XOFF, depth_z), jnp.float32)
        ],
        compiler_params=pltpu.CompilerParams(vmem_limit_bytes=48 * 1024 * 1024),
        cost_estimate=pl.CostEstimate(
            flops=60 * cur.size, bytes_accessed=4 * 6 * cur.size, transcendentals=0
        ),
    )(cur, prev, s, img, xlo, xhi, inj)


def point_tables(cell_rows, x_start, cells_wide, depth_y):
    local_x = cell_rows[0] - x_start
    inside = (local_x >= 0) & (local_x < cells_wide)
    rows_y = (cell_rows[1][:, None] == jnp.arange(depth_y, dtype=jnp.int32)[None, :]).astype(
        jnp.float32
    )
    column = local_x * 4 + cell_rows[2]
    places = (column[:, None] == jnp.arange(cells_wide * 4, dtype=jnp.int32)[None, :]) & inside[
        :, None
    ]
    return (rows_y, places.astype(jnp.float32))


def spread_points(tables, amounts, depth_z):
    rows_y, places = tables
    weighted = rows_y * amounts[:, None]
    plane = jnp.einsum("ny,nc->yc", weighted, places, precision=lax.Precision.HIGHEST)
    plane = plane.reshape(rows_y.shape[1], places.shape[1] // 4, 4)
    return jnp.pad(plane, ((0, 0), (0, 0), (0, depth_z - 4)))


def shards(older_fields, fields_now, velocity, aperture, source_pos, wavelet, receiver_pos, traces):
    slab_count = lax.axis_size("dom")
    depth_y = fields_now.shape[1]
    cells_x = fields_now.shape[2]
    depth_z = fields_now.shape[3]
    block_y = velocity.shape[0]
    steps_total = wavelet.shape[0]
    x_anchor = lax.axis_index("dom") * cells_x
    bricks = velocity.reshape(block_y, slab_count, cells_x, depth_z)
    chosen = jnp.take(bricks, aperture, axis=1)
    arrived = lax.all_to_all(chosen, "dom", split_axis=1, concat_axis=0, tiled=True)
    scaled = courant * arrived.reshape(depth_y, cells_x, depth_z)
    speed_sq = scaled * scaled
    image_zero = jnp.zeros((depth_y, cells_x, depth_z), jnp.float32)
    source_core = point_tables(source_pos, x_anchor, cells_x, depth_y)
    receiver_core = point_tables(receiver_pos, x_anchor, cells_x, depth_y)

    def advance(moment, state_carry):
        previous, current, image_acc = state_carry
        low, high = with_halo(current, "dom", 2, HALO)
        pulses = lax.dynamic_index_in_dim(wavelet, moment, 0, keepdims=False)
        recorded = lax.dynamic_index_in_dim(traces, moment, 0, keepdims=False)
        added = jnp.stack(
            [
                spread_points(source_core, pulses, depth_z),
                spread_points(receiver_core, recorded, depth_z),
            ]
        )
        updated, image_acc = step_call(current, previous, speed_sq, image_acc, low, high, added)
        return (current, updated, image_acc)

    previous, current, image_acc = lax.fori_loop(
        0, steps_total, advance, (older_fields, fields_now, image_zero)
    )
    image_acc = image_acc * (1.0 / steps_total)
    outgoing = image_acc.reshape(depth_y, 1, cells_x, depth_z)
    one_hot = (aperture[None, :] == jnp.arange(slab_count, dtype=jnp.int32)[:, None]).astype(
        jnp.float32
    )
    received = lax.all_to_all(outgoing, "dom", split_axis=0, concat_axis=1, tiled=True)
    summed = jnp.einsum("mj,yjcz->ymcz", one_hot, received, precision=lax.Precision.HIGHEST)
    image_model = summed.reshape(received.shape[0], slab_count * cells_x, received.shape[3])
    return (previous, current, image_model)


def solution(mesh):
    in_specs = (
        P(None, "survey", "dom", None),
        P(None, "survey", "dom", None),
        P("dom", "survey", None),
        P("survey"),
        P(None, "survey"),
        P(None, "survey"),
        P(None, "survey"),
        P(None, "survey"),
    )
    out_specs = (
        P(None, "survey", "dom", None),
        P(None, "survey", "dom", None),
        P("dom", "survey", None),
    )
    return jax.shard_map(shards, mesh=mesh, in_specs=in_specs, out_specs=out_specs, check_vma=False)
```

```python
import jax
import jax.numpy as jnp
from jax import lax
from jax.experimental import pallas as pl
from jax.experimental.pallas import tpu as pltpu
from jax.sharding import PartitionSpec as P

courant = 0.09
stencil_weights = (8.0 / 5.0, -1.0 / 5.0, 8.0 / 315.0, -1.0 / 560.0)
center_weight = 3.0 * (-205.0 / 72.0)
HALO = 4
XOFF = 8


def with_halo(cells, axis, dim, width):
    count = lax.axis_size(axis)
    ends = count - 1
    head = lax.slice_in_dim(cells, 0, width, axis=dim)
    tail = lax.slice_in_dim(cells, cells.shape[dim] - width, cells.shape[dim], axis=dim)
    low = lax.ppermute(tail, axis, [(i, (i + 1) % count) for i in range(ends)])
    high = lax.ppermute(head, axis, [((i + 1) % count, i) for i in range(ends)])
    return low, high


def step_kernel(
    cur_ref, prev_ref, s_ref, img_ref, xlo_ref, xhi_ref, inj_ref, out_ref, imgo_ref, ey_ref, hx_ref
):
    comps, block_y, block_x, depth_z = cur_ref.shape
    zeros_y = jnp.zeros((comps, HALO, block_x, depth_z), jnp.float32)
    ey_ref[:, 0:HALO] = zeros_y
    ey_ref[:, HALO + block_y : 2 * HALO + block_y] = zeros_y
    ey_ref[:, HALO : HALO + block_y] = cur_ref[...]
    hx_ref[0, :, :, block_x - HALO : block_x, :] = xlo_ref[...]
    hx_ref[1, :, :, 0:HALO, :] = xhi_ref[...]
    lane = lax.broadcasted_iota(jnp.int32, (block_x, depth_z), 1)
    sub = lax.broadcasted_iota(jnp.int32, (block_x, depth_z), 0)

    def row(y, carry):
        done = []
        for c in range(comps):
            ctr = ey_ref[c, HALO + y]
            left = hx_ref[0, c, y]
            right = hx_ref[1, c, y]
            acc = center_weight * ctr
            for m in range(1, HALO + 1):
                ahead = pltpu.roll(jnp.where(sub >= m, ctr, right), block_x - m, 0)
                behind = pltpu.roll(jnp.where(sub < block_x - m, ctr, left), m, 0)
                b = ahead + behind
                b = b + ey_ref[c, HALO + y + m] + ey_ref[c, HALO + y - m]
                up = jnp.where(lane < depth_z - m, pltpu.roll(ctr, depth_z - m, 1), 0.0)
                down = jnp.where(lane >= m, pltpu.roll(ctr, m, 1), 0.0)
                b = b + up + down
                acc = acc + stencil_weights[m - 1] * b
            lap = acc + inj_ref[c, y]
            upd = 2.0 * ctr - prev_ref[c, y] + s_ref[y] * lap
            out_ref[c, y] = upd
            done.append(upd)
        imgo_ref[y] = img_ref[y] + done[0] * done[1]
        return carry

    lax.fori_loop(0, block_y, row, 0, unroll=2)


def step_call(cur, prev, s, img, xlo, xhi, inj):
    comps, block_y, block_x, depth_z = cur.shape
    vmem = pl.BlockSpec(memory_space=pltpu.VMEM)
    return pl.pallas_call(
        step_kernel,
        out_shape=(
            jax.ShapeDtypeStruct(cur.shape, jnp.float32),
            jax.ShapeDtypeStruct(img.shape, jnp.float32),
        ),
        in_specs=[vmem] * 7,
        out_specs=(vmem, vmem),
        scratch_shapes=[
            pltpu.VMEM((comps, block_y + 2 * HALO, block_x, depth_z), jnp.float32),
            pltpu.VMEM((2, comps, block_y, block_x, depth_z), jnp.float32),
        ],
        input_output_aliases={1: 0, 3: 1},
        compiler_params=pltpu.CompilerParams(vmem_limit_bytes=48 * 1024 * 1024),
        cost_estimate=pl.CostEstimate(
            flops=60 * cur.size, bytes_accessed=4 * 6 * cur.size, transcendentals=0
        ),
    )(cur, prev, s, img, xlo, xhi, inj)


def point_tables(cell_rows, x_start, cells_wide, depth_y):
    local_x = cell_rows[0] - x_start
    inside = (local_x >= 0) & (local_x < cells_wide)
    rows_y = (cell_rows[1][:, None] == jnp.arange(depth_y, dtype=jnp.int32)[None, :]).astype(
        jnp.float32
    )
    column = local_x * 4 + cell_rows[2]
    places = (column[:, None] == jnp.arange(cells_wide * 4, dtype=jnp.int32)[None, :]) & inside[
        :, None
    ]
    return (rows_y, places.astype(jnp.float32))


def spread_points(tables, amounts, depth_z):
    rows_y, places = tables
    weighted = rows_y * amounts[:, None]
    plane = jnp.einsum("ny,nc->yc", weighted, places, precision=lax.Precision.HIGHEST)
    plane = plane.reshape(rows_y.shape[1], places.shape[1] // 4, 4)
    return jnp.pad(plane, ((0, 0), (0, 0), (0, depth_z - 4)))


def shards(older_fields, fields_now, velocity, aperture, source_pos, wavelet, receiver_pos, traces):
    slab_count = lax.axis_size("dom")
    depth_y = fields_now.shape[1]
    cells_x = fields_now.shape[2]
    depth_z = fields_now.shape[3]
    block_y = velocity.shape[0]
    steps_total = wavelet.shape[0]
    x_anchor = lax.axis_index("dom") * cells_x
    bricks = velocity.reshape(block_y, slab_count, cells_x, depth_z)
    chosen = jnp.take(bricks, aperture, axis=1)
    arrived = lax.all_to_all(chosen, "dom", split_axis=1, concat_axis=0, tiled=True)
    scaled = courant * arrived.reshape(depth_y, cells_x, depth_z)
    speed_sq = scaled * scaled
    image_zero = jnp.zeros((depth_y, cells_x, depth_z), jnp.float32)
    source_core = point_tables(source_pos, x_anchor, cells_x, depth_y)
    receiver_core = point_tables(receiver_pos, x_anchor, cells_x, depth_y)

    def advance(moment, previous, current, image_acc):
        low, high = with_halo(current, "dom", 2, HALO)
        pulses = lax.dynamic_index_in_dim(wavelet, moment, 0, keepdims=False)
        recorded = lax.dynamic_index_in_dim(traces, moment, 0, keepdims=False)
        added = jnp.stack(
            [
                spread_points(source_core, pulses, depth_z),
                spread_points(receiver_core, recorded, depth_z),
            ]
        )
        return step_call(current, previous, speed_sq, image_acc, low, high, added)

    def pair(index, state_carry):
        previous, current, image_acc = state_carry
        first, image_acc = advance(2 * index, previous, current, image_acc)
        second, image_acc = advance(2 * index + 1, current, first, image_acc)
        return (first, second, image_acc)

    previous, current, image_acc = lax.fori_loop(
        0, steps_total // 2, pair, (older_fields, fields_now, image_zero)
    )
    if steps_total % 2:
        last, image_acc = advance(steps_total - 1, previous, current, image_acc)
        previous, current = current, last
    image_acc = image_acc * (1.0 / steps_total)
    outgoing = image_acc.reshape(depth_y, 1, cells_x, depth_z)
    one_hot = (aperture[None, :] == jnp.arange(slab_count, dtype=jnp.int32)[:, None]).astype(
        jnp.float32
    )
    received = lax.all_to_all(outgoing, "dom", split_axis=0, concat_axis=1, tiled=True)
    summed = jnp.einsum("mj,yjcz->ymcz", one_hot, received, precision=lax.Precision.HIGHEST)
    image_model = summed.reshape(received.shape[0], slab_count * cells_x, received.shape[3])
    return (previous, current, image_model)


def solution(mesh):
    in_specs = (
        P(None, "survey", "dom", None),
        P(None, "survey", "dom", None),
        P("dom", "survey", None),
        P("survey"),
        P(None, "survey"),
        P(None, "survey"),
        P(None, "survey"),
        P(None, "survey"),
    )
    out_specs = (
        P(None, "survey", "dom", None),
        P(None, "survey", "dom", None),
        P("dom", "survey", None),
    )
    return jax.shard_map(shards, mesh=mesh, in_specs=in_specs, out_specs=out_specs, check_vma=False)
```

```python
import jax
import jax.numpy as jnp
from jax import lax
from jax.experimental import pallas as pl
from jax.experimental.pallas import tpu as pltpu
from jax.sharding import PartitionSpec as P

courant = 0.09
stencil_weights = (8.0 / 5.0, -1.0 / 5.0, 8.0 / 315.0, -1.0 / 560.0)
center_weight = 3.0 * (-205.0 / 72.0)
HALO = 4
XOFF = 8


def with_halo(cells, axis, dim, width):
    count = lax.axis_size(axis)
    ends = count - 1
    head = lax.slice_in_dim(cells, 0, width, axis=dim)
    tail = lax.slice_in_dim(cells, cells.shape[dim] - width, cells.shape[dim], axis=dim)
    low = lax.ppermute(tail, axis, [(i, (i + 1) % count) for i in range(ends)])
    high = lax.ppermute(head, axis, [((i + 1) % count, i) for i in range(ends)])
    return low, high


def step_kernel(
    moment_ref, cur_ref, prev_ref, s_ref, img_ref, xlo_ref, xhi_ref, inj_ref, out_ref, imgo_ref, ey_ref, hx_ref
):
    comps, block_y, block_x, depth_z = cur_ref.shape
    zeros_y = jnp.zeros((comps, HALO, block_x, depth_z), jnp.float32)
    ey_ref[:, 0:HALO] = zeros_y
    ey_ref[:, HALO + block_y : 2 * HALO + block_y] = zeros_y
    ey_ref[:, HALO : HALO + block_y] = cur_ref[...]
    hx_ref[0, :, :, block_x - HALO : block_x, :] = xlo_ref[...]
    hx_ref[1, :, :, 0:HALO, :] = xhi_ref[...]
    lane = lax.broadcasted_iota(jnp.int32, (block_x, depth_z), 1)
    sub = lax.broadcasted_iota(jnp.int32, (block_x, depth_z), 0)

    def row(y, carry):
        done = []
        for c in range(comps):
            ctr = ey_ref[c, HALO + y]
            left = hx_ref[0, c, y]
            right = hx_ref[1, c, y]
            acc = center_weight * ctr
            for m in range(1, HALO + 1):
                ahead = pltpu.roll(jnp.where(sub >= m, ctr, right), block_x - m, 0)
                behind = pltpu.roll(jnp.where(sub < block_x - m, ctr, left), m, 0)
                b = ahead + behind
                b = b + ey_ref[c, HALO + y + m] + ey_ref[c, HALO + y - m]
                up = jnp.where(lane < depth_z - m, pltpu.roll(ctr, depth_z - m, 1), 0.0)
                down = jnp.where(lane >= m, pltpu.roll(ctr, m, 1), 0.0)
                b = b + up + down
                acc = acc + stencil_weights[m - 1] * b
            lap = acc + inj_ref[c, y]
            upd = 2.0 * ctr - prev_ref[c, y] + s_ref[y] * lap
            out_ref[c, y] = upd
            done.append(upd)
        imgo_ref[y] = img_ref[y] + done[0] * done[1]
        return carry

    lax.fori_loop(0, block_y, row, 0, unroll=2)


def step_call(moment, cur, prev, s, img, xlo, xhi, planes):
    comps, block_y, block_x, depth_z = cur.shape

    def whole(shape):
        return pl.BlockSpec(shape, lambda i, k: (0,) * len(shape))

    plane_spec = pl.BlockSpec(
        (None, comps, block_y, block_x, depth_z), lambda i, k: (k[0], 0, 0, 0, 0)
    )
    grid_spec = pltpu.PrefetchScalarGridSpec(
        num_scalar_prefetch=1,
        grid=(1,),
        in_specs=[
            whole(cur.shape),
            whole(prev.shape),
            whole(s.shape),
            whole(img.shape),
            whole(xlo.shape),
            whole(xhi.shape),
            plane_spec,
        ],
        out_specs=(whole(cur.shape), whole(img.shape)),
        scratch_shapes=[
            pltpu.VMEM((comps, block_y + 2 * HALO, block_x, depth_z), jnp.float32),
            pltpu.VMEM((2, comps, block_y, block_x, depth_z), jnp.float32),
        ],
    )
    return pl.pallas_call(
        step_kernel,
        out_shape=(
            jax.ShapeDtypeStruct(cur.shape, jnp.float32),
            jax.ShapeDtypeStruct(img.shape, jnp.float32),
        ),
        grid_spec=grid_spec,
        input_output_aliases={2: 0, 4: 1},
        compiler_params=pltpu.CompilerParams(vmem_limit_bytes=56 * 1024 * 1024),
        cost_estimate=pl.CostEstimate(
            flops=60 * cur.size, bytes_accessed=4 * 6 * cur.size, transcendentals=0
        ),
    )(jnp.reshape(moment, (1,)).astype(jnp.int32), cur, prev, s, img, xlo, xhi, planes)


def point_tables(cell_rows, x_start, cells_wide, depth_y):
    local_x = cell_rows[0] - x_start
    inside = (local_x >= 0) & (local_x < cells_wide)
    rows_y = (cell_rows[1][:, None] == jnp.arange(depth_y, dtype=jnp.int32)[None, :]).astype(
        jnp.float32
    )
    column = local_x * 4 + cell_rows[2]
    places = (column[:, None] == jnp.arange(cells_wide * 4, dtype=jnp.int32)[None, :]) & inside[
        :, None
    ]
    return (rows_y, places.astype(jnp.float32))


def spread_points(tables, amounts, depth_z):
    rows_y, places = tables
    steps = amounts.shape[0]
    weighted = places[:, None, :] * jnp.transpose(amounts)[:, :, None]
    plane = jnp.einsum("ny,nsc->syc", rows_y, weighted, precision=lax.Precision.HIGHEST)
    plane = plane.reshape(steps, rows_y.shape[1], places.shape[1] // 4, 4)
    return jnp.pad(plane, ((0, 0), (0, 0), (0, 0), (0, depth_z - 4)))


def shards(older_fields, fields_now, velocity, aperture, source_pos, wavelet, receiver_pos, traces):
    slab_count = lax.axis_size("dom")
    depth_y = fields_now.shape[1]
    cells_x = fields_now.shape[2]
    depth_z = fields_now.shape[3]
    block_y = velocity.shape[0]
    steps_total = wavelet.shape[0]
    x_anchor = lax.axis_index("dom") * cells_x
    bricks = velocity.reshape(block_y, slab_count, cells_x, depth_z)
    chosen = jnp.take(bricks, aperture, axis=1)
    arrived = lax.all_to_all(chosen, "dom", split_axis=1, concat_axis=0, tiled=True)
    scaled = courant * arrived.reshape(depth_y, cells_x, depth_z)
    speed_sq = scaled * scaled
    image_zero = jnp.zeros((depth_y, cells_x, depth_z), jnp.float32)
    source_core = point_tables(source_pos, x_anchor, cells_x, depth_y)
    receiver_core = point_tables(receiver_pos, x_anchor, cells_x, depth_y)

    planes = jnp.stack(
        [
            spread_points(source_core, wavelet, depth_z),
            spread_points(receiver_core, traces, depth_z),
        ],
        axis=1,
    )

    def advance(moment, previous, current, image_acc):
        low, high = with_halo(current, "dom", 2, HALO)
        return step_call(moment, current, previous, speed_sq, image_acc, low, high, planes)

    def pair(index, state_carry):
        previous, current, image_acc = state_carry
        first, image_acc = advance(2 * index, previous, current, image_acc)
        second, image_acc = advance(2 * index + 1, current, first, image_acc)
        return (first, second, image_acc)

    previous, current, image_acc = lax.fori_loop(
        0, steps_total // 2, pair, (older_fields, fields_now, image_zero)
    )
    if steps_total % 2:
        last, image_acc = advance(steps_total - 1, previous, current, image_acc)
        previous, current = current, last
    image_acc = image_acc * (1.0 / steps_total)
    outgoing = image_acc.reshape(depth_y, 1, cells_x, depth_z)
    one_hot = (aperture[None, :] == jnp.arange(slab_count, dtype=jnp.int32)[:, None]).astype(
        jnp.float32
    )
    received = lax.all_to_all(outgoing, "dom", split_axis=0, concat_axis=1, tiled=True)
    summed = jnp.einsum("mj,yjcz->ymcz", one_hot, received, precision=lax.Precision.HIGHEST)
    image_model = summed.reshape(received.shape[0], slab_count * cells_x, received.shape[3])
    return (previous, current, image_model)


def solution(mesh):
    in_specs = (
        P(None, "survey", "dom", None),
        P(None, "survey", "dom", None),
        P("dom", "survey", None),
        P("survey"),
        P(None, "survey"),
        P(None, "survey"),
        P(None, "survey"),
        P(None, "survey"),
    )
    out_specs = (
        P(None, "survey", "dom", None),
        P(None, "survey", "dom", None),
        P("dom", "survey", None),
    )
    return jax.shard_map(shards, mesh=mesh, in_specs=in_specs, out_specs=out_specs, check_vma=False)
```

```python
import jax
import jax.numpy as jnp
from jax import lax
from jax.experimental import pallas as pl
from jax.experimental.pallas import tpu as pltpu
from jax.sharding import PartitionSpec as P

courant = 0.09
stencil_weights = (8.0 / 5.0, -1.0 / 5.0, 8.0 / 315.0, -1.0 / 560.0)
center_weight = 3.0 * (-205.0 / 72.0)
HALO = 4


def with_halo(cells, axis, dim, width):
    count = lax.axis_size(axis)
    ends = count - 1
    head = lax.slice_in_dim(cells, 0, width, axis=dim)
    tail = lax.slice_in_dim(cells, cells.shape[dim] - width, cells.shape[dim], axis=dim)
    low = lax.ppermute(tail, axis, [(i, (i + 1) % count) for i in range(ends)])
    high = lax.ppermute(head, axis, [((i + 1) % count, i) for i in range(ends)])
    return low, high


def step_kernel(
    moment_ref,
    cur_ref,
    prev_ref,
    s_ref,
    img_ref,
    xlo_ref,
    xhi_ref,
    ylo_ref,
    yhi_ref,
    inj_ref,
    out_ref,
    imgo_ref,
    ey_ref,
    hx_ref,
):
    comps, block_y, block_x, depth_z = cur_ref.shape
    tiles = block_x // 8
    ey_ref[:, 0:HALO] = ylo_ref[...]
    ey_ref[:, HALO + block_y : 2 * HALO + block_y] = yhi_ref[...]
    ey_ref[:, HALO : HALO + block_y] = cur_ref[...]
    hx_ref[0, :, :, 8 - HALO : 8, :] = xlo_ref[...]
    hx_ref[1, :, :, 0:HALO, :] = xhi_ref[...]
    lane = lax.broadcasted_iota(jnp.int32, (8, depth_z), 1)
    sub = lax.broadcasted_iota(jnp.int32, (8, depth_z), 0)

    def row(y, carry):
        done = []
        for c in range(comps):
            parts = [hx_ref[0, c, y]]
            for t in range(tiles):
                parts.append(ey_ref[c, HALO + y, 8 * t : 8 * t + 8])
            parts.append(hx_ref[1, c, y])
            ups = []
            for t in range(tiles):
                cols = slice(8 * t, 8 * t + 8)
                ctr = parts[t + 1]
                acc = center_weight * ctr
                for m in range(1, HALO + 1):
                    ahead = pltpu.roll(jnp.where(sub >= m, ctr, parts[t + 2]), 8 - m, 0)
                    behind = pltpu.roll(jnp.where(sub < 8 - m, ctr, parts[t]), m, 0)
                    b = ahead + behind
                    b = b + ey_ref[c, HALO + y + m, cols] + ey_ref[c, HALO + y - m, cols]
                    up = jnp.where(lane < depth_z - m, pltpu.roll(ctr, depth_z - m, 1), 0.0)
                    down = jnp.where(lane >= m, pltpu.roll(ctr, m, 1), 0.0)
                    b = b + up + down
                    acc = acc + stencil_weights[m - 1] * b
                lap = acc + inj_ref[c, y, cols]
                upd = 2.0 * ctr - prev_ref[c, y, cols] + s_ref[y, cols] * lap
                out_ref[c, y, cols] = upd
                ups.append(upd)
            done.append(ups)
        for t in range(tiles):
            cols = slice(8 * t, 8 * t + 8)
            imgo_ref[y, cols] = img_ref[y, cols] + done[0][t] * done[1][t]
        return carry

    lax.fori_loop(0, block_y, row, 0)


def step_call(moment, cur, prev, s, img, xlo, xhi, ylo, yhi, planes):
    comps, block_y, block_x, depth_z = cur.shape

    def whole(shape):
        return pl.BlockSpec(shape, lambda i, k: (0,) * len(shape))

    plane_spec = pl.BlockSpec(
        (None, comps, block_y, block_x, depth_z), lambda i, k: (k[0], 0, 0, 0, 0)
    )
    grid_spec = pltpu.PrefetchScalarGridSpec(
        num_scalar_prefetch=1,
        grid=(1,),
        in_specs=[
            whole(cur.shape),
            whole(prev.shape),
            whole(s.shape),
            whole(img.shape),
            whole(xlo.shape),
            whole(xhi.shape),
            whole(ylo.shape),
            whole(yhi.shape),
            plane_spec,
        ],
        out_specs=(whole(cur.shape), whole(img.shape)),
        scratch_shapes=[
            pltpu.VMEM((comps, block_y + 2 * HALO, block_x, depth_z), jnp.float32),
            pltpu.VMEM((2, comps, block_y, 8, depth_z), jnp.float32),
        ],
    )
    return pl.pallas_call(
        step_kernel,
        out_shape=(
            jax.ShapeDtypeStruct(cur.shape, jnp.float32),
            jax.ShapeDtypeStruct(img.shape, jnp.float32),
        ),
        grid_spec=grid_spec,
        input_output_aliases={2: 0, 4: 1},
        compiler_params=pltpu.CompilerParams(vmem_limit_bytes=56 * 1024 * 1024),
        cost_estimate=pl.CostEstimate(
            flops=60 * cur.size, bytes_accessed=4 * 6 * cur.size, transcendentals=0
        ),
    )(jnp.reshape(moment, (1,)).astype(jnp.int32), cur, prev, s, img, xlo, xhi, ylo, yhi, planes)


def group_pairs(count, pick):
    return [pair for g in range(count // 4) for pair in pick(4 * g, g)]


def to_blocks(a, count):
    member = lax.axis_index("dom") % 4
    ydim, xdim = a.ndim - 3, a.ndim - 2
    half = a.shape[ydim] // 2
    pieces = []
    for sub in range(2):
        got = []
        for h in range(2):
            part = lax.slice_in_dim(a, h * half, (h + 1) * half, axis=ydim)
            pairs = group_pairs(count, lambda b, g: [(b + 2 * e + sub, b + 2 * h + e) for e in range(2)])
            got.append(lax.ppermute(part, "dom", pairs))
        pieces.append(jnp.where(member // 2 == 0, got[0], got[1]))
    return jnp.concatenate(pieces, axis=xdim)


def from_blocks(b, count):
    member = lax.axis_index("dom") % 4
    ydim, xdim = b.ndim - 3, b.ndim - 2
    width = b.shape[xdim] // 2
    halves = []
    for h in range(2):
        got = []
        for sub in range(2):
            part = lax.slice_in_dim(b, sub * width, (sub + 1) * width, axis=xdim)
            pairs = group_pairs(count, lambda o, g: [(o + 2 * h + e, o + 2 * e + sub) for e in range(2)])
            got.append(lax.ppermute(part, "dom", pairs))
        halves.append(jnp.where(member % 2 == 0, got[0], got[1]))
    return jnp.concatenate(halves, axis=ydim)


def block_halos(cur, count):
    groups = count // 4
    low_pairs = group_pairs(count, lambda b, g: [(b + 2 * h, b + 2 * h + 1) for h in range(2)])
    low_pairs += group_pairs(
        count, lambda b, g: [(b + 2 * h + 1, b + 4 + 2 * h) for h in range(2) if g + 1 < groups]
    )
    high_pairs = [(dst, src) for src, dst in low_pairs]
    xlo = lax.ppermute(cur[:, :, -HALO:], "dom", low_pairs)
    xhi = lax.ppermute(cur[:, :, :HALO], "dom", high_pairs)
    up_pairs = group_pairs(count, lambda b, g: [(b + e, b + 2 + e) for e in range(2)])
    ylo = lax.ppermute(cur[:, -HALO:], "dom", up_pairs)
    yhi = lax.ppermute(cur[:, :HALO], "dom", [(dst, src) for src, dst in up_pairs])
    return xlo, xhi, ylo, yhi


def point_tables(cell_rows, x_start, cells_wide, y_start, depth_y):
    local_x = cell_rows[0] - x_start
    inside = (local_x >= 0) & (local_x < cells_wide)
    local_y = cell_rows[1] - y_start
    rows_y = (local_y[:, None] == jnp.arange(depth_y, dtype=jnp.int32)[None, :]).astype(
        jnp.float32
    )
    column = local_x * 4 + cell_rows[2]
    places = (column[:, None] == jnp.arange(cells_wide * 4, dtype=jnp.int32)[None, :]) & inside[
        :, None
    ]
    return (rows_y, places.astype(jnp.float32))


def spread_points(tables, amounts, depth_z):
    rows_y, places = tables
    steps = amounts.shape[0]
    weighted = places[:, None, :] * jnp.transpose(amounts)[:, :, None]
    plane = jnp.einsum("ny,nsc->syc", rows_y, weighted, precision=lax.Precision.HIGHEST)
    plane = plane.reshape(steps, rows_y.shape[1], places.shape[1] // 4, 4)
    return jnp.pad(plane, ((0, 0), (0, 0), (0, 0), (0, depth_z - 4)))


def shards(older_fields, fields_now, velocity, aperture, source_pos, wavelet, receiver_pos, traces):
    slab_count = lax.axis_size("dom")
    depth_y = fields_now.shape[1]
    cells_x = fields_now.shape[2]
    depth_z = fields_now.shape[3]
    block_y = velocity.shape[0]
    steps_total = wavelet.shape[0]
    bricks = velocity.reshape(block_y, slab_count, cells_x, depth_z)
    chosen = jnp.take(bricks, aperture, axis=1)
    arrived = lax.all_to_all(chosen, "dom", split_axis=1, concat_axis=0, tiled=True)
    scaled = courant * arrived.reshape(depth_y, cells_x, depth_z)
    speed_sq = scaled * scaled
    member = lax.axis_index("dom") % 4
    group = lax.axis_index("dom") // 4
    speed_sq = to_blocks(speed_sq, slab_count)
    older_fields = to_blocks(older_fields, slab_count)
    fields_now = to_blocks(fields_now, slab_count)
    block_rows = depth_y // 2
    block_cols = 2 * cells_x
    x_anchor = (4 * group + 2 * (member % 2)) * cells_x
    y_anchor = (member // 2) * block_rows
    image_zero = jnp.zeros((block_rows, block_cols, depth_z), jnp.float32)
    source_core = point_tables(source_pos, x_anchor, block_cols, y_anchor, block_rows)
    receiver_core = point_tables(receiver_pos, x_anchor, block_cols, y_anchor, block_rows)
    planes = jnp.stack(
        [
            spread_points(source_core, wavelet, depth_z),
            spread_points(receiver_core, traces, depth_z),
        ],
        axis=1,
    )

    def advance(moment, previous, current, image_acc):
        xlo, xhi, ylo, yhi = block_halos(current, slab_count)
        return step_call(
            moment, current, previous, speed_sq, image_acc, xlo, xhi, ylo, yhi, planes
        )

    def pair(index, state_carry):
        previous, current, image_acc = state_carry
        first, image_acc = advance(2 * index, previous, current, image_acc)
        second, image_acc = advance(2 * index + 1, current, first, image_acc)
        return (first, second, image_acc)

    previous, current, image_acc = lax.fori_loop(
        0, steps_total // 2, pair, (older_fields, fields_now, image_zero)
    )
    if steps_total % 2:
        last, image_acc = advance(steps_total - 1, previous, current, image_acc)
        previous, current = current, last
    previous = from_blocks(previous, slab_count)
    current = from_blocks(current, slab_count)
    image_acc = from_blocks(image_acc, slab_count)
    image_acc = image_acc * (1.0 / steps_total)
    outgoing = image_acc.reshape(depth_y, 1, cells_x, depth_z)
    one_hot = (aperture[None, :] == jnp.arange(slab_count, dtype=jnp.int32)[:, None]).astype(
        jnp.float32
    )
    received = lax.all_to_all(outgoing, "dom", split_axis=0, concat_axis=1, tiled=True)
    summed = jnp.einsum("mj,yjcz->ymcz", one_hot, received, precision=lax.Precision.HIGHEST)
    image_model = summed.reshape(received.shape[0], slab_count * cells_x, received.shape[3])
    return (previous, current, image_model)


def solution(mesh):
    in_specs = (
        P(None, "survey", "dom", None),
        P(None, "survey", "dom", None),
        P("dom", "survey", None),
        P("survey"),
        P(None, "survey"),
        P(None, "survey"),
        P(None, "survey"),
        P(None, "survey"),
    )
    out_specs = (
        P(None, "survey", "dom", None),
        P(None, "survey", "dom", None),
        P("dom", "survey", None),
    )
    return jax.shard_map(shards, mesh=mesh, in_specs=in_specs, out_specs=out_specs, check_vma=False)
```

```python
import jax
import jax.numpy as jnp
from jax import lax
from jax.experimental import pallas as pl
from jax.experimental.pallas import tpu as pltpu
from jax.sharding import PartitionSpec as P

courant = 0.09
stencil_weights = (8.0 / 5.0, -1.0 / 5.0, 8.0 / 315.0, -1.0 / 560.0)
center_weight = 3.0 * (-205.0 / 72.0)
HALO = 4
XOFF = 8


def trade_halos(head, tail, axis):
    count = lax.axis_size(axis)
    ends = count - 1
    low = lax.ppermute(tail, axis, [(i, (i + 1) % count) for i in range(ends)])
    high = lax.ppermute(head, axis, [((i + 1) % count, i) for i in range(ends)])
    return low, high


def step_kernel(
    moment_ref,
    cur_ref,
    prev_ref,
    s_ref,
    img_ref,
    xlo_ref,
    xhi_ref,
    inj_ref,
    out_ref,
    imgo_ref,
    head_ref,
    tail_ref,
    ey_ref,
    hx_ref,
):
    comps, block_y, block_x, depth_z = cur_ref.shape
    chunk = prev_ref.shape[1]
    index = pl.program_id(0)

    @pl.when(index == 0)
    def _():
        zeros_y = jnp.zeros((comps, HALO, block_x, depth_z), jnp.float32)
        ey_ref[:, 0:HALO] = zeros_y
        ey_ref[:, HALO + block_y : 2 * HALO + block_y] = zeros_y
        ey_ref[:, HALO : HALO + block_y] = cur_ref[...]

    hx_ref[0, :, :, block_x - HALO : block_x, :] = xlo_ref[...]
    hx_ref[1, :, :, 0:HALO, :] = xhi_ref[...]
    lane = lax.broadcasted_iota(jnp.int32, (block_x, depth_z), 1)
    sub = lax.broadcasted_iota(jnp.int32, (block_x, depth_z), 0)
    base = index * chunk

    def row(r, carry):
        y = base + r
        done = []
        for c in range(comps):
            ctr = ey_ref[c, HALO + y]
            left = hx_ref[0, c, r]
            right = hx_ref[1, c, r]
            acc = center_weight * ctr
            for m in range(1, HALO + 1):
                ahead = pltpu.roll(jnp.where(sub >= m, ctr, right), block_x - m, 0)
                behind = pltpu.roll(jnp.where(sub < block_x - m, ctr, left), m, 0)
                b = ahead + behind
                b = b + ey_ref[c, HALO + y + m] + ey_ref[c, HALO + y - m]
                up = jnp.where(lane < depth_z - m, pltpu.roll(ctr, depth_z - m, 1), 0.0)
                down = jnp.where(lane >= m, pltpu.roll(ctr, m, 1), 0.0)
                b = b + up + down
                acc = acc + stencil_weights[m - 1] * b
            lap = acc + inj_ref[c, r]
            upd = 2.0 * ctr - prev_ref[c, r] + s_ref[r] * lap
            out_ref[c, r] = upd
            head_ref[c, r] = upd[0:HALO]
            tail_ref[c, r] = upd[block_x - HALO : block_x]
            done.append(upd)
        imgo_ref[r] = img_ref[r] + done[0] * done[1]
        return carry

    lax.fori_loop(0, chunk, row, 0, unroll=2)


def step_call(moment, cur, prev, s, img, xlo, xhi, planes, chunks=8):
    comps, block_y, block_x, depth_z = cur.shape
    chunk = block_y // chunks

    def whole(shape):
        return pl.BlockSpec(shape, lambda i, k: (0,) * len(shape))

    def rows(shape):
        return pl.BlockSpec(shape, lambda i, k: (0, i) + (0,) * (len(shape) - 2))

    field_rows = rows((comps, chunk, block_x, depth_z))
    halo_rows = rows((comps, chunk, HALO, depth_z))
    flat_rows = pl.BlockSpec((chunk, block_x, depth_z), lambda i, k: (i, 0, 0))
    plane_spec = pl.BlockSpec(
        (None, comps, chunk, block_x, depth_z), lambda i, k: (k[0], 0, i, 0, 0)
    )
    grid_spec = pltpu.PrefetchScalarGridSpec(
        num_scalar_prefetch=1,
        grid=(chunks,),
        in_specs=[
            whole(cur.shape),
            field_rows,
            flat_rows,
            flat_rows,
            halo_rows,
            halo_rows,
            plane_spec,
        ],
        out_specs=(field_rows, flat_rows, halo_rows, halo_rows),
        scratch_shapes=[
            pltpu.VMEM((comps, block_y + 2 * HALO, block_x, depth_z), jnp.float32),
            pltpu.VMEM((2, comps, chunk, block_x, depth_z), jnp.float32),
        ],
    )
    halo_shape = jax.ShapeDtypeStruct((comps, block_y, HALO, depth_z), jnp.float32)
    return pl.pallas_call(
        step_kernel,
        out_shape=(
            jax.ShapeDtypeStruct(cur.shape, jnp.float32),
            jax.ShapeDtypeStruct(img.shape, jnp.float32),
            halo_shape,
            halo_shape,
        ),
        grid_spec=grid_spec,
        input_output_aliases={2: 0, 4: 1},
        compiler_params=pltpu.CompilerParams(
            dimension_semantics=("arbitrary",), vmem_limit_bytes=48 * 1024 * 1024
        ),
        cost_estimate=pl.CostEstimate(
            flops=60 * cur.size, bytes_accessed=4 * 6 * cur.size, transcendentals=0
        ),
    )(jnp.reshape(moment, (1,)).astype(jnp.int32), cur, prev, s, img, xlo, xhi, planes)


def point_tables(cell_rows, x_start, cells_wide, depth_y):
    local_x = cell_rows[0] - x_start
    inside = (local_x >= 0) & (local_x < cells_wide)
    rows_y = (cell_rows[1][:, None] == jnp.arange(depth_y, dtype=jnp.int32)[None, :]).astype(
        jnp.float32
    )
    column = local_x * 4 + cell_rows[2]
    places = (column[:, None] == jnp.arange(cells_wide * 4, dtype=jnp.int32)[None, :]) & inside[
        :, None
    ]
    return (rows_y, places.astype(jnp.float32))


def spread_points(tables, amounts):
    rows_y, places = tables
    weighted = places[:, None, :] * jnp.transpose(amounts)[:, :, None]
    return jnp.einsum("ny,nsc->syc", rows_y, weighted, precision=lax.Precision.HIGHEST)


def shards(older_fields, fields_now, velocity, aperture, source_pos, wavelet, receiver_pos, traces):
    slab_count = lax.axis_size("dom")
    depth_y = fields_now.shape[1]
    cells_x = fields_now.shape[2]
    depth_z = fields_now.shape[3]
    block_y = velocity.shape[0]
    steps_total = wavelet.shape[0]
    x_anchor = lax.axis_index("dom") * cells_x
    bricks = velocity.reshape(block_y, slab_count, cells_x, depth_z)
    chosen = jnp.take(bricks, aperture, axis=1)
    arrived = lax.all_to_all(chosen, "dom", split_axis=1, concat_axis=0, tiled=True)
    scaled = courant * arrived.reshape(depth_y, cells_x, depth_z)
    speed_sq = scaled * scaled
    image_zero = jnp.zeros((depth_y, cells_x, depth_z), jnp.float32)
    source_core = point_tables(source_pos, x_anchor, cells_x, depth_y)
    receiver_core = point_tables(receiver_pos, x_anchor, cells_x, depth_y)

    planes = jnp.stack(
        [spread_points(source_core, wavelet), spread_points(receiver_core, traces)], axis=1
    )
    planes = planes.reshape(steps_total, 2, depth_y, cells_x, 4)
    planes = jnp.pad(planes, ((0, 0), (0, 0), (0, 0), (0, 0), (0, depth_z - 4)))

    def advance(moment, previous, current, head, tail, image_acc):
        low, high = trade_halos(head, tail, "dom")
        return step_call(moment, current, previous, speed_sq, image_acc, low, high, planes)

    def pair(index, state_carry):
        previous, current, head, tail, image_acc = state_carry
        first, image_acc, head, tail = advance(2 * index, previous, current, head, tail, image_acc)
        second, image_acc, head, tail = advance(2 * index + 1, current, first, head, tail, image_acc)
        return (first, second, head, tail, image_acc)

    start = (
        older_fields,
        fields_now,
        fields_now[:, :, :HALO],
        fields_now[:, :, cells_x - HALO :],
        image_zero,
    )
    previous, current, head, tail, image_acc = lax.fori_loop(0, steps_total // 2, pair, start)
    if steps_total % 2:
        last, image_acc, head, tail = advance(
            steps_total - 1, previous, current, head, tail, image_acc
        )
        previous, current = current, last
    image_acc = image_acc * (1.0 / steps_total)
    outgoing = image_acc.reshape(depth_y, 1, cells_x, depth_z)
    one_hot = (aperture[None, :] == jnp.arange(slab_count, dtype=jnp.int32)[:, None]).astype(
        jnp.float32
    )
    received = lax.all_to_all(outgoing, "dom", split_axis=0, concat_axis=1, tiled=True)
    summed = jnp.einsum("mj,yjcz->ymcz", one_hot, received, precision=lax.Precision.HIGHEST)
    image_model = summed.reshape(received.shape[0], slab_count * cells_x, received.shape[3])
    return (previous, current, image_model)


def solution(mesh):
    in_specs = (
        P(None, "survey", "dom", None),
        P(None, "survey", "dom", None),
        P("dom", "survey", None),
        P("survey"),
        P(None, "survey"),
        P(None, "survey"),
        P(None, "survey"),
        P(None, "survey"),
    )
    out_specs = (
        P(None, "survey", "dom", None),
        P(None, "survey", "dom", None),
        P("dom", "survey", None),
    )
    return jax.shard_map(shards, mesh=mesh, in_specs=in_specs, out_specs=out_specs, check_vma=False)
```

```python
import functools

import jax
import jax.numpy as jnp
from jax import lax
from jax.experimental import pallas as pl
from jax.experimental.pallas import tpu as pltpu
from jax.sharding import PartitionSpec as P

courant = 0.09
stencil_weights = (8.0 / 5.0, -1.0 / 5.0, 8.0 / 315.0, -1.0 / 560.0)
center_weight = 3.0 * (-205.0 / 72.0)
HALO = 4
XOFF = 8


def trade_halos(head, tail, axis):
    count = lax.axis_size(axis)
    ends = count - 1
    low = lax.ppermute(tail, axis, [(i, (i + 1) % count) for i in range(ends)])
    high = lax.ppermute(head, axis, [((i + 1) % count, i) for i in range(ends)])
    return low, high


def wave_kernel(with_image, moment_ref, cur_ref, prev_ref, s_ref, xlo_ref, xhi_ref, inj_ref, *rest):
    if with_image:
        other_ref, img_ref, out_ref, head_ref, tail_ref, imgo_ref, ey_ref, hx_ref = rest
    else:
        out_ref, head_ref, tail_ref, ey_ref, hx_ref = rest
    block_y, block_x, depth_z = cur_ref.shape
    zeros_y = jnp.zeros((HALO, block_x, depth_z), jnp.float32)
    ey_ref[0:HALO] = zeros_y
    ey_ref[HALO + block_y : 2 * HALO + block_y] = zeros_y
    ey_ref[HALO : HALO + block_y] = cur_ref[...]
    hx_ref[0, :, block_x - HALO : block_x, :] = xlo_ref[...]
    hx_ref[1, :, 0:HALO, :] = xhi_ref[...]
    lane = lax.broadcasted_iota(jnp.int32, (block_x, depth_z), 1)
    sub = lax.broadcasted_iota(jnp.int32, (block_x, depth_z), 0)

    def row(y, carry):
        ctr = ey_ref[HALO + y]
        left = hx_ref[0, y]
        right = hx_ref[1, y]
        acc = center_weight * ctr
        for m in range(1, HALO + 1):
            ahead = pltpu.roll(jnp.where(sub >= m, ctr, right), block_x - m, 0)
            behind = pltpu.roll(jnp.where(sub < block_x - m, ctr, left), m, 0)
            b = ahead + behind
            b = b + ey_ref[HALO + y + m] + ey_ref[HALO + y - m]
            up = jnp.where(lane < depth_z - m, pltpu.roll(ctr, depth_z - m, 1), 0.0)
            down = jnp.where(lane >= m, pltpu.roll(ctr, m, 1), 0.0)
            b = b + up + down
            acc = acc + stencil_weights[m - 1] * b
        lap = acc + inj_ref[y]
        upd = 2.0 * ctr - prev_ref[y] + s_ref[y] * lap
        out_ref[y] = upd
        head_ref[y] = upd[0:HALO]
        tail_ref[y] = upd[block_x - HALO : block_x]
        if with_image:
            imgo_ref[y] = img_ref[y] + other_ref[y] * upd
        return carry

    lax.fori_loop(0, block_y, row, 0, unroll=2)


def wave_call(component, moment, cur, prev, s, xlo, xhi, planes, other=None, img=None):
    block_y, block_x, depth_z = cur.shape
    with_image = img is not None

    def whole(shape):
        return pl.BlockSpec(shape, lambda i, k: (0,) * len(shape))

    plane_spec = pl.BlockSpec(
        (None, None, block_y, block_x, depth_z), lambda i, k: (k[0], component, 0, 0, 0)
    )
    in_specs = [whole(cur.shape), whole(prev.shape), whole(s.shape), whole(xlo.shape), whole(xhi.shape), plane_spec]
    operands = [cur, prev, s, xlo, xhi, planes]
    halo_shape = jax.ShapeDtypeStruct(xlo.shape, jnp.float32)
    out_shape = [jax.ShapeDtypeStruct(cur.shape, jnp.float32), halo_shape, halo_shape]
    out_specs = [whole(cur.shape), whole(xlo.shape), whole(xlo.shape)]
    aliases = {2: 0}
    if with_image:
        in_specs += [whole(other.shape), whole(img.shape)]
        operands += [other, img]
        out_shape.append(jax.ShapeDtypeStruct(img.shape, jnp.float32))
        out_specs.append(whole(img.shape))
        aliases[8] = 3
    grid_spec = pltpu.PrefetchScalarGridSpec(
        num_scalar_prefetch=1,
        grid=(1,),
        in_specs=in_specs,
        out_specs=tuple(out_specs),
        scratch_shapes=[
            pltpu.VMEM((block_y + 2 * HALO, block_x, depth_z), jnp.float32),
            pltpu.VMEM((2, block_y, block_x, depth_z), jnp.float32),
        ],
    )
    return pl.pallas_call(
        functools.partial(wave_kernel, with_image),
        out_shape=tuple(out_shape),
        grid_spec=grid_spec,
        input_output_aliases=aliases,
        compiler_params=pltpu.CompilerParams(vmem_limit_bytes=48 * 1024 * 1024),
        cost_estimate=pl.CostEstimate(
            flops=60 * cur.size, bytes_accessed=4 * 6 * cur.size, transcendentals=0
        ),
    )(jnp.reshape(moment, (1,)).astype(jnp.int32), *operands)


def point_tables(cell_rows, x_start, cells_wide, depth_y):
    local_x = cell_rows[0] - x_start
    inside = (local_x >= 0) & (local_x < cells_wide)
    rows_y = (cell_rows[1][:, None] == jnp.arange(depth_y, dtype=jnp.int32)[None, :]).astype(
        jnp.float32
    )
    column = local_x * 4 + cell_rows[2]
    places = (column[:, None] == jnp.arange(cells_wide * 4, dtype=jnp.int32)[None, :]) & inside[
        :, None
    ]
    return (rows_y, places.astype(jnp.float32))


def spread_points(tables, amounts):
    rows_y, places = tables
    weighted = places[:, None, :] * jnp.transpose(amounts)[:, :, None]
    return jnp.einsum("ny,nsc->syc", rows_y, weighted, precision=lax.Precision.HIGHEST)


def shards(older_fields, fields_now, velocity, aperture, source_pos, wavelet, receiver_pos, traces):
    slab_count = lax.axis_size("dom")
    depth_y = fields_now.shape[1]
    cells_x = fields_now.shape[2]
    depth_z = fields_now.shape[3]
    block_y = velocity.shape[0]
    steps_total = wavelet.shape[0]
    x_anchor = lax.axis_index("dom") * cells_x
    bricks = velocity.reshape(block_y, slab_count, cells_x, depth_z)
    chosen = jnp.take(bricks, aperture, axis=1)
    arrived = lax.all_to_all(chosen, "dom", split_axis=1, concat_axis=0, tiled=True)
    scaled = courant * arrived.reshape(depth_y, cells_x, depth_z)
    speed_sq = scaled * scaled
    image_zero = jnp.zeros((depth_y, cells_x, depth_z), jnp.float32)
    source_core = point_tables(source_pos, x_anchor, cells_x, depth_y)
    receiver_core = point_tables(receiver_pos, x_anchor, cells_x, depth_y)

    planes = jnp.stack(
        [spread_points(source_core, wavelet), spread_points(receiver_core, traces)], axis=1
    )
    planes = planes.reshape(steps_total, 2, depth_y, cells_x, 4)
    planes = jnp.pad(planes, ((0, 0), (0, 0), (0, 0), (0, 0), (0, depth_z - 4)))

    def advance(moment, state):
        (prev0, cur0, head0, tail0), (prev1, cur1, head1, tail1), image_acc = state
        low0, high0 = trade_halos(head0, tail0, "dom")
        low1, high1 = trade_halos(head1, tail1, "dom")
        new0, head0, tail0 = wave_call(0, moment, cur0, prev0, speed_sq, low0, high0, planes)
        new1, head1, tail1, image_acc = wave_call(
            1, moment, cur1, prev1, speed_sq, low1, high1, planes, new0, image_acc
        )
        return (cur0, new0, head0, tail0), (cur1, new1, head1, tail1), image_acc

    def pair(index, state):
        return advance(2 * index + 1, advance(2 * index, state))

    def edges(field):
        return (field[:, :HALO], field[:, cells_x - HALO :])

    start = (
        (older_fields[0], fields_now[0]) + edges(fields_now[0]),
        (older_fields[1], fields_now[1]) + edges(fields_now[1]),
        image_zero,
    )
    state = lax.fori_loop(0, steps_total // 2, pair, start)
    if steps_total % 2:
        state = advance(steps_total - 1, state)
    (prev0, cur0, _, _), (prev1, cur1, _, _), image_acc = state
    previous = jnp.stack([prev0, prev1])
    current = jnp.stack([cur0, cur1])
    image_acc = image_acc * (1.0 / steps_total)
    outgoing = image_acc.reshape(depth_y, 1, cells_x, depth_z)
    one_hot = (aperture[None, :] == jnp.arange(slab_count, dtype=jnp.int32)[:, None]).astype(
        jnp.float32
    )
    received = lax.all_to_all(outgoing, "dom", split_axis=0, concat_axis=1, tiled=True)
    summed = jnp.einsum("mj,yjcz->ymcz", one_hot, received, precision=lax.Precision.HIGHEST)
    image_model = summed.reshape(received.shape[0], slab_count * cells_x, received.shape[3])
    return (previous, current, image_model)


def solution(mesh):
    in_specs = (
        P(None, "survey", "dom", None),
        P(None, "survey", "dom", None),
        P("dom", "survey", None),
        P("survey"),
        P(None, "survey"),
        P(None, "survey"),
        P(None, "survey"),
        P(None, "survey"),
    )
    out_specs = (
        P(None, "survey", "dom", None),
        P(None, "survey", "dom", None),
        P("dom", "survey", None),
    )
    return jax.shard_map(shards, mesh=mesh, in_specs=in_specs, out_specs=out_specs, check_vma=False)
```

```python
import functools

import jax
import jax.numpy as jnp
from jax import lax
from jax.experimental import pallas as pl
from jax.experimental.pallas import tpu as pltpu
from jax.sharding import PartitionSpec as P

courant = 0.09
stencil_weights = (8.0 / 5.0, -1.0 / 5.0, 8.0 / 315.0, -1.0 / 560.0)
center_weight = 3.0 * (-205.0 / 72.0)
HALO = 4
ROWS = 8
XOFF = 8


def trade_halos(head, tail, axis):
    count = lax.axis_size(axis)
    ends = count - 1
    low = lax.ppermute(tail, axis, [(i, (i + 1) % count) for i in range(ends)])
    high = lax.ppermute(head, axis, [((i + 1) % count, i) for i in range(ends)])
    return low, high


def wave_kernel(with_image, moment_ref, cur_ref, prev_ref, s_ref, xlo_ref, xhi_ref, inj_ref, *rest):
    if with_image:
        other_ref, img_ref, out_ref, head_ref, tail_ref, imgo_ref, ey_ref, hx_ref = rest
    else:
        out_ref, head_ref, tail_ref, ey_ref, hx_ref = rest
    block_y, block_x, depth_z = cur_ref.shape
    zeros_y = jnp.zeros((HALO, block_x, depth_z), jnp.float32)
    ey_ref[0:HALO] = zeros_y
    ey_ref[HALO + block_y : 2 * HALO + block_y] = zeros_y
    ey_ref[HALO : HALO + block_y] = cur_ref[...]
    hx_ref[0, :, block_x - HALO : block_x, :] = xlo_ref[...]
    hx_ref[1, :, 0:HALO, :] = xhi_ref[...]
    rows = ROWS
    lane = lax.broadcasted_iota(jnp.int32, (rows, block_x, depth_z), 2)
    sub = lax.broadcasted_iota(jnp.int32, (rows, block_x, depth_z), 1)

    def chunk(index, carry):
        y = pl.multiple_of(index * rows, rows)
        ctr = ey_ref[pl.ds(HALO + y, rows)]
        left = hx_ref[0, pl.ds(y, rows)]
        right = hx_ref[1, pl.ds(y, rows)]
        acc = center_weight * ctr
        for m in range(1, HALO + 1):
            ahead = pltpu.roll(jnp.where(sub >= m, ctr, right), block_x - m, 1)
            behind = pltpu.roll(jnp.where(sub < block_x - m, ctr, left), m, 1)
            b = ahead + behind
            b = b + ey_ref[pl.ds(HALO + y + m, rows)] + ey_ref[pl.ds(HALO + y - m, rows)]
            up = jnp.where(lane < depth_z - m, pltpu.roll(ctr, depth_z - m, 2), 0.0)
            down = jnp.where(lane >= m, pltpu.roll(ctr, m, 2), 0.0)
            b = b + up + down
            acc = acc + stencil_weights[m - 1] * b
        lap = acc + inj_ref[pl.ds(y, rows)]
        upd = 2.0 * ctr - prev_ref[pl.ds(y, rows)] + s_ref[pl.ds(y, rows)] * lap
        out_ref[pl.ds(y, rows)] = upd
        head_ref[pl.ds(y, rows)] = upd[:, 0:HALO]
        tail_ref[pl.ds(y, rows)] = upd[:, block_x - HALO : block_x]
        if with_image:
            imgo_ref[pl.ds(y, rows)] = img_ref[pl.ds(y, rows)] + other_ref[pl.ds(y, rows)] * upd
        return carry

    lax.fori_loop(0, block_y // rows, chunk, 0)


def wave_call(component, moment, cur, prev, s, xlo, xhi, planes, other=None, img=None):
    block_y, block_x, depth_z = cur.shape
    with_image = img is not None

    def whole(shape):
        return pl.BlockSpec(shape, lambda i, k: (0,) * len(shape))

    plane_spec = pl.BlockSpec(
        (None, None, block_y, block_x, depth_z), lambda i, k: (k[0], component, 0, 0, 0)
    )
    in_specs = [whole(cur.shape), whole(prev.shape), whole(s.shape), whole(xlo.shape), whole(xhi.shape), plane_spec]
    operands = [cur, prev, s, xlo, xhi, planes]
    halo_shape = jax.ShapeDtypeStruct(xlo.shape, jnp.float32)
    out_shape = [jax.ShapeDtypeStruct(cur.shape, jnp.float32), halo_shape, halo_shape]
    out_specs = [whole(cur.shape), whole(xlo.shape), whole(xlo.shape)]
    aliases = {2: 0}
    if with_image:
        in_specs += [whole(other.shape), whole(img.shape)]
        operands += [other, img]
        out_shape.append(jax.ShapeDtypeStruct(img.shape, jnp.float32))
        out_specs.append(whole(img.shape))
        aliases[8] = 3
    grid_spec = pltpu.PrefetchScalarGridSpec(
        num_scalar_prefetch=1,
        grid=(1,),
        in_specs=in_specs,
        out_specs=tuple(out_specs),
        scratch_shapes=[
            pltpu.VMEM((block_y + 2 * HALO, block_x, depth_z), jnp.float32),
            pltpu.VMEM((2, block_y, block_x, depth_z), jnp.float32),
        ],
    )
    return pl.pallas_call(
        functools.partial(wave_kernel, with_image),
        out_shape=tuple(out_shape),
        grid_spec=grid_spec,
        input_output_aliases=aliases,
        compiler_params=pltpu.CompilerParams(vmem_limit_bytes=48 * 1024 * 1024),
        cost_estimate=pl.CostEstimate(
            flops=60 * cur.size, bytes_accessed=4 * 6 * cur.size, transcendentals=0
        ),
    )(jnp.reshape(moment, (1,)).astype(jnp.int32), *operands)


def point_tables(cell_rows, x_start, cells_wide, depth_y):
    local_x = cell_rows[0] - x_start
    inside = (local_x >= 0) & (local_x < cells_wide)
    rows_y = (cell_rows[1][:, None] == jnp.arange(depth_y, dtype=jnp.int32)[None, :]).astype(
        jnp.float32
    )
    column = local_x * 4 + cell_rows[2]
    places = (column[:, None] == jnp.arange(cells_wide * 4, dtype=jnp.int32)[None, :]) & inside[
        :, None
    ]
    return (rows_y, places.astype(jnp.float32))


def spread_points(tables, amounts):
    rows_y, places = tables
    weighted = places[:, None, :] * jnp.transpose(amounts)[:, :, None]
    return jnp.einsum("ny,nsc->syc", rows_y, weighted, precision=lax.Precision.HIGHEST)


def shards(older_fields, fields_now, velocity, aperture, source_pos, wavelet, receiver_pos, traces):
    slab_count = lax.axis_size("dom")
    depth_y = fields_now.shape[1]
    cells_x = fields_now.shape[2]
    depth_z = fields_now.shape[3]
    block_y = velocity.shape[0]
    steps_total = wavelet.shape[0]
    x_anchor = lax.axis_index("dom") * cells_x
    bricks = velocity.reshape(block_y, slab_count, cells_x, depth_z)
    chosen = jnp.take(bricks, aperture, axis=1)
    arrived = lax.all_to_all(chosen, "dom", split_axis=1, concat_axis=0, tiled=True)
    scaled = courant * arrived.reshape(depth_y, cells_x, depth_z)
    speed_sq = scaled * scaled
    image_zero = jnp.zeros((depth_y, cells_x, depth_z), jnp.float32)
    source_core = point_tables(source_pos, x_anchor, cells_x, depth_y)
    receiver_core = point_tables(receiver_pos, x_anchor, cells_x, depth_y)

    planes = jnp.stack(
        [spread_points(source_core, wavelet), spread_points(receiver_core, traces)], axis=1
    )
    planes = planes.reshape(steps_total, 2, depth_y, cells_x, 4)
    planes = jnp.pad(planes, ((0, 0), (0, 0), (0, 0), (0, 0), (0, depth_z - 4)))

    def advance(moment, state):
        (prev0, cur0, head0, tail0), (prev1, cur1, head1, tail1), image_acc = state
        low0, high0 = trade_halos(head0, tail0, "dom")
        low1, high1 = trade_halos(head1, tail1, "dom")
        new0, head0, tail0 = wave_call(0, moment, cur0, prev0, speed_sq, low0, high0, planes)
        new1, head1, tail1, image_acc = wave_call(
            1, moment, cur1, prev1, speed_sq, low1, high1, planes, new0, image_acc
        )
        return (cur0, new0, head0, tail0), (cur1, new1, head1, tail1), image_acc

    def pair(index, state):
        return advance(2 * index + 1, advance(2 * index, state))

    def edges(field):
        return (field[:, :HALO], field[:, cells_x - HALO :])

    start = (
        (older_fields[0], fields_now[0]) + edges(fields_now[0]),
        (older_fields[1], fields_now[1]) + edges(fields_now[1]),
        image_zero,
    )
    state = lax.fori_loop(0, steps_total // 2, pair, start)
    if steps_total % 2:
        state = advance(steps_total - 1, state)
    (prev0, cur0, _, _), (prev1, cur1, _, _), image_acc = state
    previous = jnp.stack([prev0, prev1])
    current = jnp.stack([cur0, cur1])
    image_acc = image_acc * (1.0 / steps_total)
    outgoing = image_acc.reshape(depth_y, 1, cells_x, depth_z)
    one_hot = (aperture[None, :] == jnp.arange(slab_count, dtype=jnp.int32)[:, None]).astype(
        jnp.float32
    )
    received = lax.all_to_all(outgoing, "dom", split_axis=0, concat_axis=1, tiled=True)
    summed = jnp.einsum("mj,yjcz->ymcz", one_hot, received, precision=lax.Precision.HIGHEST)
    image_model = summed.reshape(received.shape[0], slab_count * cells_x, received.shape[3])
    return (previous, current, image_model)


def solution(mesh):
    in_specs = (
        P(None, "survey", "dom", None),
        P(None, "survey", "dom", None),
        P("dom", "survey", None),
        P("survey"),
        P(None, "survey"),
        P(None, "survey"),
        P(None, "survey"),
        P(None, "survey"),
    )
    out_specs = (
        P(None, "survey", "dom", None),
        P(None, "survey", "dom", None),
        P("dom", "survey", None),
    )
    return jax.shard_map(shards, mesh=mesh, in_specs=in_specs, out_specs=out_specs, check_vma=False)
```

```python
import functools

import jax
import jax.numpy as jnp
from jax import lax
from jax.experimental import pallas as pl
from jax.experimental.pallas import tpu as pltpu
from jax.sharding import PartitionSpec as P

courant = 0.09
stencil_weights = (8.0 / 5.0, -1.0 / 5.0, 8.0 / 315.0, -1.0 / 560.0)
center_weight = 3.0 * (-205.0 / 72.0)
HALO = 4
ROWS = 8
XOFF = 8


def trade_halos(head, tail, axis):
    count = lax.axis_size(axis)
    ends = count - 1
    low = lax.ppermute(tail, axis, [(i, (i + 1) % count) for i in range(ends)])
    high = lax.ppermute(head, axis, [((i + 1) % count, i) for i in range(ends)])
    return low, high


def wave_kernel(with_image, moment_ref, cur_ref, prev_ref, s_ref, xlo_ref, xhi_ref, inj_ref, *rest):
    if with_image:
        other_ref, img_ref, out_ref, head_ref, tail_ref, imgo_ref, ey_ref, hx_ref = rest
    else:
        out_ref, head_ref, tail_ref, ey_ref, hx_ref = rest
    block_y, block_x, depth_z = cur_ref.shape
    zeros_y = jnp.zeros((HALO, block_x, depth_z), jnp.float32)
    ey_ref[0:HALO] = zeros_y
    ey_ref[HALO + block_y : 2 * HALO + block_y] = zeros_y
    ey_ref[HALO : HALO + block_y] = cur_ref[...]
    hx_ref[0, :, block_x - HALO : block_x, :] = xlo_ref[...]
    hx_ref[1, :, 0:HALO, :] = xhi_ref[...]
    rows = ROWS
    lane = lax.broadcasted_iota(jnp.int32, (rows, block_x, depth_z), 2)
    sub = lax.broadcasted_iota(jnp.int32, (rows, block_x, depth_z), 1)

    def chunk(index, carry):
        y = pl.multiple_of(index * rows, rows)
        ctr = ey_ref[pl.ds(HALO + y, rows)]
        left = hx_ref[0, pl.ds(y, rows)]
        right = hx_ref[1, pl.ds(y, rows)]
        acc = center_weight * ctr
        for m in range(1, HALO + 1):
            ahead = pltpu.roll(jnp.where(sub >= m, ctr, right), block_x - m, 1)
            behind = pltpu.roll(jnp.where(sub < block_x - m, ctr, left), m, 1)
            b = ahead + behind
            b = b + ey_ref[pl.ds(HALO + y + m, rows)] + ey_ref[pl.ds(HALO + y - m, rows)]
            up = jnp.where(lane < depth_z - m, pltpu.roll(ctr, depth_z - m, 2), 0.0)
            down = jnp.where(lane >= m, pltpu.roll(ctr, m, 2), 0.0)
            b = b + up + down
            acc = acc + stencil_weights[m - 1] * b
        spread = jnp.broadcast_to(inj_ref[pl.ds(y, rows)], (rows, block_x, depth_z))
        spread = pltpu.roll(spread, 0, 2, stride=4, stride_axis=1)
        lap = acc + jnp.where(lane < 4, spread, 0.0)
        upd = 2.0 * ctr - prev_ref[pl.ds(y, rows)] + s_ref[pl.ds(y, rows)] * lap
        out_ref[pl.ds(y, rows)] = upd
        head_ref[pl.ds(y, rows)] = upd[:, 0:HALO]
        tail_ref[pl.ds(y, rows)] = upd[:, block_x - HALO : block_x]
        if with_image:
            imgo_ref[pl.ds(y, rows)] = img_ref[pl.ds(y, rows)] + other_ref[pl.ds(y, rows)] * upd
        return carry

    lax.fori_loop(0, block_y // rows, chunk, 0)


def wave_call(component, moment, cur, prev, s, xlo, xhi, planes, other=None, img=None):
    block_y, block_x, depth_z = cur.shape
    with_image = img is not None

    def whole(shape):
        return pl.BlockSpec(shape, lambda i, k: (0,) * len(shape))

    plane_spec = pl.BlockSpec(
        (None, None, block_y, 1, depth_z), lambda i, k: (k[0], component, 0, 0, 0)
    )
    in_specs = [whole(cur.shape), whole(prev.shape), whole(s.shape), whole(xlo.shape), whole(xhi.shape), plane_spec]
    operands = [cur, prev, s, xlo, xhi, planes]
    halo_shape = jax.ShapeDtypeStruct(xlo.shape, jnp.float32)
    out_shape = [jax.ShapeDtypeStruct(cur.shape, jnp.float32), halo_shape, halo_shape]
    out_specs = [whole(cur.shape), whole(xlo.shape), whole(xlo.shape)]
    aliases = {2: 0}
    if with_image:
        in_specs += [whole(other.shape), whole(img.shape)]
        operands += [other, img]
        out_shape.append(jax.ShapeDtypeStruct(img.shape, jnp.float32))
        out_specs.append(whole(img.shape))
        aliases[8] = 3
    grid_spec = pltpu.PrefetchScalarGridSpec(
        num_scalar_prefetch=1,
        grid=(1,),
        in_specs=in_specs,
        out_specs=tuple(out_specs),
        scratch_shapes=[
            pltpu.VMEM((block_y + 2 * HALO, block_x, depth_z), jnp.float32),
            pltpu.VMEM((2, block_y, block_x, depth_z), jnp.float32),
        ],
    )
    return pl.pallas_call(
        functools.partial(wave_kernel, with_image),
        out_shape=tuple(out_shape),
        grid_spec=grid_spec,
        input_output_aliases=aliases,
        compiler_params=pltpu.CompilerParams(vmem_limit_bytes=48 * 1024 * 1024),
        cost_estimate=pl.CostEstimate(
            flops=60 * cur.size, bytes_accessed=4 * 6 * cur.size, transcendentals=0
        ),
    )(jnp.reshape(moment, (1,)).astype(jnp.int32), *operands)


def point_tables(cell_rows, x_start, cells_wide, depth_y):
    local_x = cell_rows[0] - x_start
    inside = (local_x >= 0) & (local_x < cells_wide)
    rows_y = (cell_rows[1][:, None] == jnp.arange(depth_y, dtype=jnp.int32)[None, :]).astype(
        jnp.float32
    )
    column = local_x * 4 + cell_rows[2]
    places = (column[:, None] == jnp.arange(cells_wide * 4, dtype=jnp.int32)[None, :]) & inside[
        :, None
    ]
    return (rows_y, places.astype(jnp.float32))


def spread_points(tables, amounts):
    rows_y, places = tables
    weighted = places[:, None, :] * jnp.transpose(amounts)[:, :, None]
    return jnp.einsum("ny,nsc->syc", rows_y, weighted, precision=lax.Precision.HIGHEST)


def shards(older_fields, fields_now, velocity, aperture, source_pos, wavelet, receiver_pos, traces):
    slab_count = lax.axis_size("dom")
    depth_y = fields_now.shape[1]
    cells_x = fields_now.shape[2]
    depth_z = fields_now.shape[3]
    block_y = velocity.shape[0]
    steps_total = wavelet.shape[0]
    x_anchor = lax.axis_index("dom") * cells_x
    bricks = velocity.reshape(block_y, slab_count, cells_x, depth_z)
    chosen = jnp.take(bricks, aperture, axis=1)
    arrived = lax.all_to_all(chosen, "dom", split_axis=1, concat_axis=0, tiled=True)
    scaled = courant * arrived.reshape(depth_y, cells_x, depth_z)
    speed_sq = scaled * scaled
    image_zero = jnp.zeros((depth_y, cells_x, depth_z), jnp.float32)
    source_core = point_tables(source_pos, x_anchor, cells_x, depth_y)
    receiver_core = point_tables(receiver_pos, x_anchor, cells_x, depth_y)

    planes = jnp.stack(
        [spread_points(source_core, wavelet), spread_points(receiver_core, traces)], axis=1
    )
    planes = planes.reshape(steps_total, 2, depth_y, cells_x, 4)
    gap = jnp.zeros((steps_total, 2, depth_y, depth_z - 4 * cells_x), jnp.float32)
    tail = planes[:, :, :, :0:-1].reshape(steps_total, 2, depth_y, 4 * (cells_x - 1))
    planes = jnp.concatenate([planes[:, :, :, 0], gap, tail], axis=3)
    planes = planes.reshape(steps_total, 2, depth_y, 1, depth_z)

    def advance(moment, state):
        (prev0, cur0, head0, tail0), (prev1, cur1, head1, tail1), image_acc = state
        low0, high0 = trade_halos(head0, tail0, "dom")
        low1, high1 = trade_halos(head1, tail1, "dom")
        new0, head0, tail0 = wave_call(0, moment, cur0, prev0, speed_sq, low0, high0, planes)
        new1, head1, tail1, image_acc = wave_call(
            1, moment, cur1, prev1, speed_sq, low1, high1, planes, new0, image_acc
        )
        return (cur0, new0, head0, tail0), (cur1, new1, head1, tail1), image_acc

    def pair(index, state):
        return advance(2 * index + 1, advance(2 * index, state))

    def edges(field):
        return (field[:, :HALO], field[:, cells_x - HALO :])

    start = (
        (older_fields[0], fields_now[0]) + edges(fields_now[0]),
        (older_fields[1], fields_now[1]) + edges(fields_now[1]),
        image_zero,
    )
    state = lax.fori_loop(0, steps_total // 2, pair, start)
    if steps_total % 2:
        state = advance(steps_total - 1, state)
    (prev0, cur0, _, _), (prev1, cur1, _, _), image_acc = state
    previous = jnp.stack([prev0, prev1])
    current = jnp.stack([cur0, cur1])
    image_acc = image_acc * (1.0 / steps_total)
    outgoing = image_acc.reshape(depth_y, 1, cells_x, depth_z)
    one_hot = (aperture[None, :] == jnp.arange(slab_count, dtype=jnp.int32)[:, None]).astype(
        jnp.float32
    )
    received = lax.all_to_all(outgoing, "dom", split_axis=0, concat_axis=1, tiled=True)
    summed = jnp.einsum("mj,yjcz->ymcz", one_hot, received, precision=lax.Precision.HIGHEST)
    image_model = summed.reshape(received.shape[0], slab_count * cells_x, received.shape[3])
    return (previous, current, image_model)


def solution(mesh):
    in_specs = (
        P(None, "survey", "dom", None),
        P(None, "survey", "dom", None),
        P("dom", "survey", None),
        P("survey"),
        P(None, "survey"),
        P(None, "survey"),
        P(None, "survey"),
        P(None, "survey"),
    )
    out_specs = (
        P(None, "survey", "dom", None),
        P(None, "survey", "dom", None),
        P("dom", "survey", None),
    )
    return jax.shard_map(shards, mesh=mesh, in_specs=in_specs, out_specs=out_specs, check_vma=False)
```

```python
import functools

import jax
import jax.numpy as jnp
from jax import lax
from jax.experimental import pallas as pl
from jax.experimental.pallas import tpu as pltpu
from jax.sharding import PartitionSpec as P

courant = 0.09
stencil_weights = (8.0 / 5.0, -1.0 / 5.0, 8.0 / 315.0, -1.0 / 560.0)
center_weight = 3.0 * (-205.0 / 72.0)
HALO = 4
ROWS = 8
PARTS = 4
XOFF = 8


def trade_halos(head, tail, axis):
    count = lax.axis_size(axis)
    ends = count - 1
    low = lax.ppermute(tail, axis, [(i, (i + 1) % count) for i in range(ends)])
    high = lax.ppermute(head, axis, [((i + 1) % count, i) for i in range(ends)])
    return low, high


def wave_kernel(with_image, moment_ref, cur_ref, prev_ref, s_ref, xlo_ref, xhi_ref, inj_ref, *rest):
    if with_image:
        other_ref, img_ref, out_ref, head_ref, tail_ref, imgo_ref, ey_ref, hx_ref = rest
    else:
        out_ref, head_ref, tail_ref, ey_ref, hx_ref = rest
    block_y, block_x, depth_z = cur_ref.shape
    part = prev_ref.shape[0]
    index = pl.program_id(0)

    @pl.when(index == 0)
    def _():
        zeros_y = jnp.zeros((HALO, block_x, depth_z), jnp.float32)
        ey_ref[0:HALO] = zeros_y
        ey_ref[HALO + block_y : 2 * HALO + block_y] = zeros_y
        ey_ref[HALO : HALO + block_y] = cur_ref[...]

    hx_ref[0, :, block_x - HALO : block_x, :] = xlo_ref[...]
    hx_ref[1, :, 0:HALO, :] = xhi_ref[...]
    rows = ROWS
    base = index * part
    lane = lax.broadcasted_iota(jnp.int32, (rows, block_x, depth_z), 2)
    sub = lax.broadcasted_iota(jnp.int32, (rows, block_x, depth_z), 1)

    def chunk(step, carry):
        r = pl.multiple_of(step * rows, rows)
        y = base + r
        ctr = ey_ref[pl.ds(HALO + y, rows)]
        left = hx_ref[0, pl.ds(r, rows)]
        right = hx_ref[1, pl.ds(r, rows)]
        acc = center_weight * ctr
        for m in range(1, HALO + 1):
            ahead = pltpu.roll(jnp.where(sub >= m, ctr, right), block_x - m, 1)
            behind = pltpu.roll(jnp.where(sub < block_x - m, ctr, left), m, 1)
            b = ahead + behind
            b = b + ey_ref[pl.ds(HALO + y + m, rows)] + ey_ref[pl.ds(HALO + y - m, rows)]
            up = jnp.where(lane < depth_z - m, pltpu.roll(ctr, depth_z - m, 2), 0.0)
            down = jnp.where(lane >= m, pltpu.roll(ctr, m, 2), 0.0)
            b = b + up + down
            acc = acc + stencil_weights[m - 1] * b
        spread = jnp.broadcast_to(inj_ref[pl.ds(r, rows)], (rows, block_x, depth_z))
        spread = pltpu.roll(spread, 0, 2, stride=4, stride_axis=1)
        lap = acc + jnp.where(lane < 4, spread, 0.0)
        upd = 2.0 * ctr - prev_ref[pl.ds(r, rows)] + s_ref[pl.ds(r, rows)] * lap
        out_ref[pl.ds(r, rows)] = upd
        head_ref[pl.ds(r, rows)] = upd[:, 0:HALO]
        tail_ref[pl.ds(r, rows)] = upd[:, block_x - HALO : block_x]
        if with_image:
            imgo_ref[pl.ds(r, rows)] = img_ref[pl.ds(r, rows)] + other_ref[pl.ds(r, rows)] * upd
        return carry

    lax.fori_loop(0, part // rows, chunk, 0)


def wave_call(component, moment, cur, prev, s, xlo, xhi, planes, other=None, img=None):
    block_y, block_x, depth_z = cur.shape
    with_image = img is not None
    parts = PARTS
    part = block_y // parts

    def whole(shape):
        return pl.BlockSpec(shape, lambda i, k: (0,) * len(shape))

    def chunked(shape):
        return pl.BlockSpec((part,) + shape[1:], lambda i, k: (i,) + (0,) * (len(shape) - 1))

    plane_spec = pl.BlockSpec(
        (None, None, part, 1, depth_z), lambda i, k: (k[0], component, i, 0, 0)
    )
    in_specs = [
        whole(cur.shape),
        chunked(prev.shape),
        chunked(s.shape),
        chunked(xlo.shape),
        chunked(xhi.shape),
        plane_spec,
    ]
    operands = [cur, prev, s, xlo, xhi, planes]
    halo_shape = jax.ShapeDtypeStruct(xlo.shape, jnp.float32)
    out_shape = [jax.ShapeDtypeStruct(cur.shape, jnp.float32), halo_shape, halo_shape]
    out_specs = [chunked(cur.shape), chunked(xlo.shape), chunked(xlo.shape)]
    aliases = {2: 0}
    if with_image:
        in_specs += [chunked(other.shape), chunked(img.shape)]
        operands += [other, img]
        out_shape.append(jax.ShapeDtypeStruct(img.shape, jnp.float32))
        out_specs.append(chunked(img.shape))
        aliases[8] = 3
    grid_spec = pltpu.PrefetchScalarGridSpec(
        num_scalar_prefetch=1,
        grid=(parts,),
        in_specs=in_specs,
        out_specs=tuple(out_specs),
        scratch_shapes=[
            pltpu.VMEM((block_y + 2 * HALO, block_x, depth_z), jnp.float32),
            pltpu.VMEM((2, part, block_x, depth_z), jnp.float32),
        ],
    )
    return pl.pallas_call(
        functools.partial(wave_kernel, with_image),
        out_shape=tuple(out_shape),
        grid_spec=grid_spec,
        input_output_aliases=aliases,
        compiler_params=pltpu.CompilerParams(
            dimension_semantics=("arbitrary",), vmem_limit_bytes=48 * 1024 * 1024
        ),
        cost_estimate=pl.CostEstimate(
            flops=60 * cur.size, bytes_accessed=4 * 6 * cur.size, transcendentals=0
        ),
    )(jnp.reshape(moment, (1,)).astype(jnp.int32), *operands)


def point_tables(cell_rows, x_start, cells_wide, depth_y):
    local_x = cell_rows[0] - x_start
    inside = (local_x >= 0) & (local_x < cells_wide)
    rows_y = (cell_rows[1][:, None] == jnp.arange(depth_y, dtype=jnp.int32)[None, :]).astype(
        jnp.float32
    )
    column = local_x * 4 + cell_rows[2]
    places = (column[:, None] == jnp.arange(cells_wide * 4, dtype=jnp.int32)[None, :]) & inside[
        :, None
    ]
    return (rows_y, places.astype(jnp.float32))


def spread_points(tables, amounts):
    rows_y, places = tables
    weighted = places[:, None, :] * jnp.transpose(amounts)[:, :, None]
    return jnp.einsum("ny,nsc->syc", rows_y, weighted, precision=lax.Precision.HIGHEST)


def shards(older_fields, fields_now, velocity, aperture, source_pos, wavelet, receiver_pos, traces):
    slab_count = lax.axis_size("dom")
    depth_y = fields_now.shape[1]
    cells_x = fields_now.shape[2]
    depth_z = fields_now.shape[3]
    block_y = velocity.shape[0]
    steps_total = wavelet.shape[0]
    x_anchor = lax.axis_index("dom") * cells_x
    bricks = velocity.reshape(block_y, slab_count, cells_x, depth_z)
    chosen = jnp.take(bricks, aperture, axis=1)
    arrived = lax.all_to_all(chosen, "dom", split_axis=1, concat_axis=0, tiled=True)
    scaled = courant * arrived.reshape(depth_y, cells_x, depth_z)
    speed_sq = scaled * scaled
    image_zero = jnp.zeros((depth_y, cells_x, depth_z), jnp.float32)
    source_core = point_tables(source_pos, x_anchor, cells_x, depth_y)
    receiver_core = point_tables(receiver_pos, x_anchor, cells_x, depth_y)

    planes = jnp.stack(
        [spread_points(source_core, wavelet), spread_points(receiver_core, traces)], axis=1
    )
    planes = planes.reshape(steps_total, 2, depth_y, cells_x, 4)
    gap = jnp.zeros((steps_total, 2, depth_y, depth_z - 4 * cells_x), jnp.float32)
    tail = planes[:, :, :, :0:-1].reshape(steps_total, 2, depth_y, 4 * (cells_x - 1))
    planes = jnp.concatenate([planes[:, :, :, 0], gap, tail], axis=3)
    planes = planes.reshape(steps_total, 2, depth_y, 1, depth_z)

    def advance(moment, state):
        (prev0, cur0, head0, tail0), (prev1, cur1, head1, tail1), image_acc = state
        low0, high0 = trade_halos(head0, tail0, "dom")
        low1, high1 = trade_halos(head1, tail1, "dom")
        new0, head0, tail0 = wave_call(0, moment, cur0, prev0, speed_sq, low0, high0, planes)
        new1, head1, tail1, image_acc = wave_call(
            1, moment, cur1, prev1, speed_sq, low1, high1, planes, new0, image_acc
        )
        return (cur0, new0, head0, tail0), (cur1, new1, head1, tail1), image_acc

    def pair(index, state):
        return advance(2 * index + 1, advance(2 * index, state))

    def edges(field):
        return (field[:, :HALO], field[:, cells_x - HALO :])

    start = (
        (older_fields[0], fields_now[0]) + edges(fields_now[0]),
        (older_fields[1], fields_now[1]) + edges(fields_now[1]),
        image_zero,
    )
    state = lax.fori_loop(0, steps_total // 2, pair, start)
    if steps_total % 2:
        state = advance(steps_total - 1, state)
    (prev0, cur0, _, _), (prev1, cur1, _, _), image_acc = state
    previous = jnp.stack([prev0, prev1])
    current = jnp.stack([cur0, cur1])
    image_acc = image_acc * (1.0 / steps_total)
    outgoing = image_acc.reshape(depth_y, 1, cells_x, depth_z)
    one_hot = (aperture[None, :] == jnp.arange(slab_count, dtype=jnp.int32)[:, None]).astype(
        jnp.float32
    )
    received = lax.all_to_all(outgoing, "dom", split_axis=0, concat_axis=1, tiled=True)
    summed = jnp.einsum("mj,yjcz->ymcz", one_hot, received, precision=lax.Precision.HIGHEST)
    image_model = summed.reshape(received.shape[0], slab_count * cells_x, received.shape[3])
    return (previous, current, image_model)


def solution(mesh):
    in_specs = (
        P(None, "survey", "dom", None),
        P(None, "survey", "dom", None),
        P("dom", "survey", None),
        P("survey"),
        P(None, "survey"),
        P(None, "survey"),
        P(None, "survey"),
        P(None, "survey"),
    )
    out_specs = (
        P(None, "survey", "dom", None),
        P(None, "survey", "dom", None),
        P("dom", "survey", None),
    )
    return jax.shard_map(shards, mesh=mesh, in_specs=in_specs, out_specs=out_specs, check_vma=False)
```

```python
import functools

import jax
import jax.numpy as jnp
from jax import lax
from jax.experimental import pallas as pl
from jax.experimental.pallas import tpu as pltpu
from jax.sharding import PartitionSpec as P

courant = 0.09
stencil_weights = (8.0 / 5.0, -1.0 / 5.0, 8.0 / 315.0, -1.0 / 560.0)
center_weight = 3.0 * (-205.0 / 72.0)
HALO = 4
ROWS = 4
XOFF = 8


def trade_halos(head, tail, axis):
    count = lax.axis_size(axis)
    ends = count - 1
    low = lax.ppermute(tail, axis, [(i, (i + 1) % count) for i in range(ends)])
    high = lax.ppermute(head, axis, [((i + 1) % count, i) for i in range(ends)])
    return low, high


def wave_kernel(with_image, moment_ref, cur_ref, prev_ref, s_ref, xlo_ref, xhi_ref, inj_ref, *rest):
    if with_image:
        other_ref, img_ref, out_ref, head_ref, tail_ref, imgo_ref, ey_ref, hx_ref = rest
    else:
        out_ref, head_ref, tail_ref, ey_ref, hx_ref = rest
    block_y, block_x, depth_z = cur_ref.shape
    zeros_y = jnp.zeros((HALO, block_x, depth_z), jnp.float32)
    ey_ref[0:HALO] = zeros_y
    ey_ref[HALO + block_y : 2 * HALO + block_y] = zeros_y
    ey_ref[HALO : HALO + block_y] = cur_ref[...]
    hx_ref[0, :, block_x - HALO : block_x, :] = xlo_ref[...]
    hx_ref[1, :, 0:HALO, :] = xhi_ref[...]
    rows = ROWS
    lane = lax.broadcasted_iota(jnp.int32, (rows, block_x, depth_z), 2)
    sub = lax.broadcasted_iota(jnp.int32, (rows, block_x, depth_z), 1)

    def chunk(index, carry):
        y = pl.multiple_of(index * rows, rows)
        ctr = ey_ref[pl.ds(HALO + y, rows)]
        left = hx_ref[0, pl.ds(y, rows)]
        right = hx_ref[1, pl.ds(y, rows)]
        acc = center_weight * ctr
        for m in range(1, HALO + 1):
            ahead = pltpu.roll(jnp.where(sub >= m, ctr, right), block_x - m, 1)
            behind = pltpu.roll(jnp.where(sub < block_x - m, ctr, left), m, 1)
            b = ahead + behind
            b = b + ey_ref[pl.ds(HALO + y + m, rows)] + ey_ref[pl.ds(HALO + y - m, rows)]
            up = jnp.where(lane < depth_z - m, pltpu.roll(ctr, depth_z - m, 2), 0.0)
            down = jnp.where(lane >= m, pltpu.roll(ctr, m, 2), 0.0)
            b = b + up + down
            acc = acc + stencil_weights[m - 1] * b
        spread = jnp.broadcast_to(inj_ref[pl.ds(y, rows)], (rows, block_x, depth_z))
        spread = pltpu.roll(spread, 0, 2, stride=4, stride_axis=1)
        lap = acc + jnp.where(lane < 4, spread, 0.0)
        upd = 2.0 * ctr - prev_ref[pl.ds(y, rows)] + s_ref[pl.ds(y, rows)] * lap
        out_ref[pl.ds(y, rows)] = upd
        head_ref[pl.ds(y, rows)] = upd[:, 0:HALO]
        tail_ref[pl.ds(y, rows)] = upd[:, block_x - HALO : block_x]
        if with_image:
            imgo_ref[pl.ds(y, rows)] = img_ref[pl.ds(y, rows)] + other_ref[pl.ds(y, rows)] * upd
        return carry

    lax.fori_loop(0, block_y // rows, chunk, 0)


def wave_call(component, moment, cur, prev, s, xlo, xhi, planes, other=None, img=None):
    block_y, block_x, depth_z = cur.shape
    with_image = img is not None

    def whole(shape):
        return pl.BlockSpec(shape, lambda i, k: (0,) * len(shape))

    plane_spec = pl.BlockSpec(
        (None, None, block_y, 1, depth_z), lambda i, k: (k[0], component, 0, 0, 0)
    )
    in_specs = [whole(cur.shape), whole(prev.shape), whole(s.shape), whole(xlo.shape), whole(xhi.shape), plane_spec]
    operands = [cur, prev, s, xlo, xhi, planes]
    halo_shape = jax.ShapeDtypeStruct(xlo.shape, jnp.float32)
    out_shape = [jax.ShapeDtypeStruct(cur.shape, jnp.float32), halo_shape, halo_shape]
    out_specs = [whole(cur.shape), whole(xlo.shape), whole(xlo.shape)]
    aliases = {2: 0}
    if with_image:
        in_specs += [whole(other.shape), whole(img.shape)]
        operands += [other, img]
        out_shape.append(jax.ShapeDtypeStruct(img.shape, jnp.float32))
        out_specs.append(whole(img.shape))
        aliases[8] = 3
    grid_spec = pltpu.PrefetchScalarGridSpec(
        num_scalar_prefetch=1,
        grid=(1,),
        in_specs=in_specs,
        out_specs=tuple(out_specs),
        scratch_shapes=[
            pltpu.VMEM((block_y + 2 * HALO, block_x, depth_z), jnp.float32),
            pltpu.VMEM((2, block_y, block_x, depth_z), jnp.float32),
        ],
    )
    return pl.pallas_call(
        functools.partial(wave_kernel, with_image),
        out_shape=tuple(out_shape),
        grid_spec=grid_spec,
        input_output_aliases=aliases,
        compiler_params=pltpu.CompilerParams(vmem_limit_bytes=48 * 1024 * 1024),
        cost_estimate=pl.CostEstimate(
            flops=60 * cur.size, bytes_accessed=4 * 6 * cur.size, transcendentals=0
        ),
    )(jnp.reshape(moment, (1,)).astype(jnp.int32), *operands)


def point_tables(cell_rows, x_start, cells_wide, depth_y):
    local_x = cell_rows[0] - x_start
    inside = (local_x >= 0) & (local_x < cells_wide)
    rows_y = (cell_rows[1][:, None] == jnp.arange(depth_y, dtype=jnp.int32)[None, :]).astype(
        jnp.float32
    )
    column = local_x * 4 + cell_rows[2]
    places = (column[:, None] == jnp.arange(cells_wide * 4, dtype=jnp.int32)[None, :]) & inside[
        :, None
    ]
    return (rows_y, places.astype(jnp.float32))


def spread_points(tables, amounts):
    rows_y, places = tables
    weighted = places[:, None, :] * jnp.transpose(amounts)[:, :, None]
    return jnp.einsum("ny,nsc->syc", rows_y, weighted, precision=lax.Precision.HIGHEST)


def shards(older_fields, fields_now, velocity, aperture, source_pos, wavelet, receiver_pos, traces):
    slab_count = lax.axis_size("dom")
    depth_y = fields_now.shape[1]
    cells_x = fields_now.shape[2]
    depth_z = fields_now.shape[3]
    block_y = velocity.shape[0]
    steps_total = wavelet.shape[0]
    x_anchor = lax.axis_index("dom") * cells_x
    bricks = velocity.reshape(block_y, slab_count, cells_x, depth_z)
    chosen = jnp.take(bricks, aperture, axis=1)
    arrived = lax.all_to_all(chosen, "dom", split_axis=1, concat_axis=0, tiled=True)
    scaled = courant * arrived.reshape(depth_y, cells_x, depth_z)
    speed_sq = scaled * scaled
    image_zero = jnp.zeros((depth_y, cells_x, depth_z), jnp.float32)
    source_core = point_tables(source_pos, x_anchor, cells_x, depth_y)
    receiver_core = point_tables(receiver_pos, x_anchor, cells_x, depth_y)

    planes = jnp.stack(
        [spread_points(source_core, wavelet), spread_points(receiver_core, traces)], axis=1
    )
    planes = planes.reshape(steps_total, 2, depth_y, cells_x, 4)
    gap = jnp.zeros((steps_total, 2, depth_y, depth_z - 4 * cells_x), jnp.float32)
    tail = planes[:, :, :, :0:-1].reshape(steps_total, 2, depth_y, 4 * (cells_x - 1))
    planes = jnp.concatenate([planes[:, :, :, 0], gap, tail], axis=3)
    planes = planes.reshape(steps_total, 2, depth_y, 1, depth_z)

    def advance(moment, state):
        (prev0, cur0, head0, tail0), (prev1, cur1, head1, tail1), image_acc = state
        low0, high0 = trade_halos(head0, tail0, "dom")
        low1, high1 = trade_halos(head1, tail1, "dom")
        new0, head0, tail0 = wave_call(0, moment, cur0, prev0, speed_sq, low0, high0, planes)
        new1, head1, tail1, image_acc = wave_call(
            1, moment, cur1, prev1, speed_sq, low1, high1, planes, new0, image_acc
        )
        return (cur0, new0, head0, tail0), (cur1, new1, head1, tail1), image_acc

    def pair(index, state):
        return advance(2 * index + 1, advance(2 * index, state))

    def edges(field):
        return (field[:, :HALO], field[:, cells_x - HALO :])

    start = (
        (older_fields[0], fields_now[0]) + edges(fields_now[0]),
        (older_fields[1], fields_now[1]) + edges(fields_now[1]),
        image_zero,
    )
    state = lax.fori_loop(0, steps_total // 2, pair, start)
    if steps_total % 2:
        state = advance(steps_total - 1, state)
    (prev0, cur0, _, _), (prev1, cur1, _, _), image_acc = state
    previous = jnp.stack([prev0, prev1])
    current = jnp.stack([cur0, cur1])
    image_acc = image_acc * (1.0 / steps_total)
    outgoing = image_acc.reshape(depth_y, 1, cells_x, depth_z)
    one_hot = (aperture[None, :] == jnp.arange(slab_count, dtype=jnp.int32)[:, None]).astype(
        jnp.float32
    )
    received = lax.all_to_all(outgoing, "dom", split_axis=0, concat_axis=1, tiled=True)
    summed = jnp.einsum("mj,yjcz->ymcz", one_hot, received, precision=lax.Precision.HIGHEST)
    image_model = summed.reshape(received.shape[0], slab_count * cells_x, received.shape[3])
    return (previous, current, image_model)


def solution(mesh):
    in_specs = (
        P(None, "survey", "dom", None),
        P(None, "survey", "dom", None),
        P("dom", "survey", None),
        P("survey"),
        P(None, "survey"),
        P(None, "survey"),
        P(None, "survey"),
        P(None, "survey"),
    )
    out_specs = (
        P(None, "survey", "dom", None),
        P(None, "survey", "dom", None),
        P("dom", "survey", None),
    )
    return jax.shard_map(shards, mesh=mesh, in_specs=in_specs, out_specs=out_specs, check_vma=False)
```

```python
import functools

import jax
import jax.numpy as jnp
from jax import lax
from jax.experimental import pallas as pl
from jax.experimental.pallas import tpu as pltpu
from jax.sharding import PartitionSpec as P

courant = 0.09
stencil_weights = (8.0 / 5.0, -1.0 / 5.0, 8.0 / 315.0, -1.0 / 560.0)
center_weight = 3.0 * (-205.0 / 72.0)
HALO = 4
ROWS = 16
XOFF = 8


def trade_halos(head, tail, axis):
    count = lax.axis_size(axis)
    ends = count - 1
    low = lax.ppermute(tail, axis, [(i, (i + 1) % count) for i in range(ends)])
    high = lax.ppermute(head, axis, [((i + 1) % count, i) for i in range(ends)])
    return low, high


def wave_kernel(with_image, moment_ref, cur_ref, prev_ref, s_ref, xlo_ref, xhi_ref, inj_ref, *rest):
    if with_image:
        other_ref, img_ref, out_ref, head_ref, tail_ref, imgo_ref, ey_ref, hx_ref = rest
    else:
        out_ref, head_ref, tail_ref, ey_ref, hx_ref = rest
    block_y, block_x, depth_z = cur_ref.shape
    zeros_y = jnp.zeros((HALO, block_x, depth_z), jnp.float32)
    ey_ref[0:HALO] = zeros_y
    ey_ref[HALO + block_y : 2 * HALO + block_y] = zeros_y
    ey_ref[HALO : HALO + block_y] = cur_ref[...]
    hx_ref[0, :, block_x - HALO : block_x, :] = xlo_ref[...]
    hx_ref[1, :, 0:HALO, :] = xhi_ref[...]
    rows = ROWS
    lane = lax.broadcasted_iota(jnp.int32, (rows, block_x, depth_z), 2)
    sub = lax.broadcasted_iota(jnp.int32, (rows, block_x, depth_z), 1)

    def chunk(index, carry):
        y = pl.multiple_of(index * rows, rows)
        ctr = ey_ref[pl.ds(HALO + y, rows)]
        left = hx_ref[0, pl.ds(y, rows)]
        right = hx_ref[1, pl.ds(y, rows)]
        acc = center_weight * ctr
        for m in range(1, HALO + 1):
            ahead = pltpu.roll(jnp.where(sub >= m, ctr, right), block_x - m, 1)
            behind = pltpu.roll(jnp.where(sub < block_x - m, ctr, left), m, 1)
            b = ahead + behind
            b = b + ey_ref[pl.ds(HALO + y + m, rows)] + ey_ref[pl.ds(HALO + y - m, rows)]
            up = jnp.where(lane < depth_z - m, pltpu.roll(ctr, depth_z - m, 2), 0.0)
            down = jnp.where(lane >= m, pltpu.roll(ctr, m, 2), 0.0)
            b = b + up + down
            acc = acc + stencil_weights[m - 1] * b
        spread = jnp.broadcast_to(inj_ref[pl.ds(y, rows)], (rows, block_x, depth_z))
        spread = pltpu.roll(spread, 0, 2, stride=4, stride_axis=1)
        lap = acc + jnp.where(lane < 4, spread, 0.0)
        upd = 2.0 * ctr - prev_ref[pl.ds(y, rows)] + s_ref[pl.ds(y, rows)] * lap
        out_ref[pl.ds(y, rows)] = upd
        head_ref[pl.ds(y, rows)] = upd[:, 0:HALO]
        tail_ref[pl.ds(y, rows)] = upd[:, block_x - HALO : block_x]
        if with_image:
            imgo_ref[pl.ds(y, rows)] = img_ref[pl.ds(y, rows)] + other_ref[pl.ds(y, rows)] * upd
        return carry

    lax.fori_loop(0, block_y // rows, chunk, 0)


def wave_call(component, moment, cur, prev, s, xlo, xhi, planes, other=None, img=None):
    block_y, block_x, depth_z = cur.shape
    with_image = img is not None

    def whole(shape):
        return pl.BlockSpec(shape, lambda i, k: (0,) * len(shape))

    plane_spec = pl.BlockSpec(
        (None, None, block_y, 1, depth_z), lambda i, k: (k[0], component, 0, 0, 0)
    )
    in_specs = [whole(cur.shape), whole(prev.shape), whole(s.shape), whole(xlo.shape), whole(xhi.shape), plane_spec]
    operands = [cur, prev, s, xlo, xhi, planes]
    halo_shape = jax.ShapeDtypeStruct(xlo.shape, jnp.float32)
    out_shape = [jax.ShapeDtypeStruct(cur.shape, jnp.float32), halo_shape, halo_shape]
    out_specs = [whole(cur.shape), whole(xlo.shape), whole(xlo.shape)]
    aliases = {2: 0}
    if with_image:
        in_specs += [whole(other.shape), whole(img.shape)]
        operands += [other, img]
        out_shape.append(jax.ShapeDtypeStruct(img.shape, jnp.float32))
        out_specs.append(whole(img.shape))
        aliases[8] = 3
    grid_spec = pltpu.PrefetchScalarGridSpec(
        num_scalar_prefetch=1,
        grid=(1,),
        in_specs=in_specs,
        out_specs=tuple(out_specs),
        scratch_shapes=[
            pltpu.VMEM((block_y + 2 * HALO, block_x, depth_z), jnp.float32),
            pltpu.VMEM((2, block_y, block_x, depth_z), jnp.float32),
        ],
    )
    return pl.pallas_call(
        functools.partial(wave_kernel, with_image),
        out_shape=tuple(out_shape),
        grid_spec=grid_spec,
        input_output_aliases=aliases,
        compiler_params=pltpu.CompilerParams(vmem_limit_bytes=48 * 1024 * 1024),
        cost_estimate=pl.CostEstimate(
            flops=60 * cur.size, bytes_accessed=4 * 6 * cur.size, transcendentals=0
        ),
    )(jnp.reshape(moment, (1,)).astype(jnp.int32), *operands)


def point_tables(cell_rows, x_start, cells_wide, depth_y):
    local_x = cell_rows[0] - x_start
    inside = (local_x >= 0) & (local_x < cells_wide)
    rows_y = (cell_rows[1][:, None] == jnp.arange(depth_y, dtype=jnp.int32)[None, :]).astype(
        jnp.float32
    )
    column = local_x * 4 + cell_rows[2]
    places = (column[:, None] == jnp.arange(cells_wide * 4, dtype=jnp.int32)[None, :]) & inside[
        :, None
    ]
    return (rows_y, places.astype(jnp.float32))


def spread_points(tables, amounts):
    rows_y, places = tables
    weighted = places[:, None, :] * jnp.transpose(amounts)[:, :, None]
    return jnp.einsum("ny,nsc->syc", rows_y, weighted, precision=lax.Precision.HIGHEST)


def shards(older_fields, fields_now, velocity, aperture, source_pos, wavelet, receiver_pos, traces):
    slab_count = lax.axis_size("dom")
    depth_y = fields_now.shape[1]
    cells_x = fields_now.shape[2]
    depth_z = fields_now.shape[3]
    block_y = velocity.shape[0]
    steps_total = wavelet.shape[0]
    x_anchor = lax.axis_index("dom") * cells_x
    bricks = velocity.reshape(block_y, slab_count, cells_x, depth_z)
    chosen = jnp.take(bricks, aperture, axis=1)
    arrived = lax.all_to_all(chosen, "dom", split_axis=1, concat_axis=0, tiled=True)
    scaled = courant * arrived.reshape(depth_y, cells_x, depth_z)
    speed_sq = scaled * scaled
    image_zero = jnp.zeros((depth_y, cells_x, depth_z), jnp.float32)
    source_core = point_tables(source_pos, x_anchor, cells_x, depth_y)
    receiver_core = point_tables(receiver_pos, x_anchor, cells_x, depth_y)

    planes = jnp.stack(
        [spread_points(source_core, wavelet), spread_points(receiver_core, traces)], axis=1
    )
    planes = planes.reshape(steps_total, 2, depth_y, cells_x, 4)
    gap = jnp.zeros((steps_total, 2, depth_y, depth_z - 4 * cells_x), jnp.float32)
    tail = planes[:, :, :, :0:-1].reshape(steps_total, 2, depth_y, 4 * (cells_x - 1))
    planes = jnp.concatenate([planes[:, :, :, 0], gap, tail], axis=3)
    planes = planes.reshape(steps_total, 2, depth_y, 1, depth_z)

    def advance(moment, state):
        (prev0, cur0, head0, tail0), (prev1, cur1, head1, tail1), image_acc = state
        low0, high0 = trade_halos(head0, tail0, "dom")
        low1, high1 = trade_halos(head1, tail1, "dom")
        new0, head0, tail0 = wave_call(0, moment, cur0, prev0, speed_sq, low0, high0, planes)
        new1, head1, tail1, image_acc = wave_call(
            1, moment, cur1, prev1, speed_sq, low1, high1, planes, new0, image_acc
        )
        return (cur0, new0, head0, tail0), (cur1, new1, head1, tail1), image_acc

    def pair(index, state):
        return advance(2 * index + 1, advance(2 * index, state))

    def edges(field):
        return (field[:, :HALO], field[:, cells_x - HALO :])

    start = (
        (older_fields[0], fields_now[0]) + edges(fields_now[0]),
        (older_fields[1], fields_now[1]) + edges(fields_now[1]),
        image_zero,
    )
    state = lax.fori_loop(0, steps_total // 2, pair, start)
    if steps_total % 2:
        state = advance(steps_total - 1, state)
    (prev0, cur0, _, _), (prev1, cur1, _, _), image_acc = state
    previous = jnp.stack([prev0, prev1])
    current = jnp.stack([cur0, cur1])
    image_acc = image_acc * (1.0 / steps_total)
    outgoing = image_acc.reshape(depth_y, 1, cells_x, depth_z)
    one_hot = (aperture[None, :] == jnp.arange(slab_count, dtype=jnp.int32)[:, None]).astype(
        jnp.float32
    )
    received = lax.all_to_all(outgoing, "dom", split_axis=0, concat_axis=1, tiled=True)
    summed = jnp.einsum("mj,yjcz->ymcz", one_hot, received, precision=lax.Precision.HIGHEST)
    image_model = summed.reshape(received.shape[0], slab_count * cells_x, received.shape[3])
    return (previous, current, image_model)


def solution(mesh):
    in_specs = (
        P(None, "survey", "dom", None),
        P(None, "survey", "dom", None),
        P("dom", "survey", None),
        P("survey"),
        P(None, "survey"),
        P(None, "survey"),
        P(None, "survey"),
        P(None, "survey"),
    )
    out_specs = (
        P(None, "survey", "dom", None),
        P(None, "survey", "dom", None),
        P("dom", "survey", None),
    )
    return jax.shard_map(shards, mesh=mesh, in_specs=in_specs, out_specs=out_specs, check_vma=False)
```

```python
import functools

import jax
import jax.numpy as jnp
from jax import lax
from jax.experimental import pallas as pl
from jax.experimental.pallas import tpu as pltpu
from jax.sharding import PartitionSpec as P

courant = 0.09
stencil_weights = (8.0 / 5.0, -1.0 / 5.0, 8.0 / 315.0, -1.0 / 560.0)
center_weight = 3.0 * (-205.0 / 72.0)
HALO = 4
ROWS = 32
XOFF = 8


def trade_halos(head, tail, axis):
    count = lax.axis_size(axis)
    ends = count - 1
    low = lax.ppermute(tail, axis, [(i, (i + 1) % count) for i in range(ends)])
    high = lax.ppermute(head, axis, [((i + 1) % count, i) for i in range(ends)])
    return low, high


def wave_kernel(with_image, moment_ref, cur_ref, prev_ref, s_ref, xlo_ref, xhi_ref, inj_ref, *rest):
    if with_image:
        other_ref, img_ref, out_ref, head_ref, tail_ref, imgo_ref, ey_ref, hx_ref = rest
    else:
        out_ref, head_ref, tail_ref, ey_ref, hx_ref = rest
    block_y, block_x, depth_z = cur_ref.shape
    zeros_y = jnp.zeros((HALO, block_x, depth_z), jnp.float32)
    ey_ref[0:HALO] = zeros_y
    ey_ref[HALO + block_y : 2 * HALO + block_y] = zeros_y
    ey_ref[HALO : HALO + block_y] = cur_ref[...]
    hx_ref[0, :, block_x - HALO : block_x, :] = xlo_ref[...]
    hx_ref[1, :, 0:HALO, :] = xhi_ref[...]
    rows = ROWS
    lane = lax.broadcasted_iota(jnp.int32, (rows, block_x, depth_z), 2)
    sub = lax.broadcasted_iota(jnp.int32, (rows, block_x, depth_z), 1)

    def chunk(index, carry):
        y = pl.multiple_of(index * rows, rows)
        ctr = ey_ref[pl.ds(HALO + y, rows)]
        left = hx_ref[0, pl.ds(y, rows)]
        right = hx_ref[1, pl.ds(y, rows)]
        acc = center_weight * ctr
        for m in range(1, HALO + 1):
            ahead = pltpu.roll(jnp.where(sub >= m, ctr, right), block_x - m, 1)
            behind = pltpu.roll(jnp.where(sub < block_x - m, ctr, left), m, 1)
            b = ahead + behind
            b = b + ey_ref[pl.ds(HALO + y + m, rows)] + ey_ref[pl.ds(HALO + y - m, rows)]
            up = jnp.where(lane < depth_z - m, pltpu.roll(ctr, depth_z - m, 2), 0.0)
            down = jnp.where(lane >= m, pltpu.roll(ctr, m, 2), 0.0)
            b = b + up + down
            acc = acc + stencil_weights[m - 1] * b
        spread = jnp.broadcast_to(inj_ref[pl.ds(y, rows)], (rows, block_x, depth_z))
        spread = pltpu.roll(spread, 0, 2, stride=4, stride_axis=1)
        lap = acc + jnp.where(lane < 4, spread, 0.0)
        upd = 2.0 * ctr - prev_ref[pl.ds(y, rows)] + s_ref[pl.ds(y, rows)] * lap
        out_ref[pl.ds(y, rows)] = upd
        head_ref[pl.ds(y, rows)] = upd[:, 0:HALO]
        tail_ref[pl.ds(y, rows)] = upd[:, block_x - HALO : block_x]
        if with_image:
            imgo_ref[pl.ds(y, rows)] = img_ref[pl.ds(y, rows)] + other_ref[pl.ds(y, rows)] * upd
        return carry

    lax.fori_loop(0, block_y // rows, chunk, 0)


def wave_call(component, moment, cur, prev, s, xlo, xhi, planes, other=None, img=None):
    block_y, block_x, depth_z = cur.shape
    with_image = img is not None

    def whole(shape):
        return pl.BlockSpec(shape, lambda i, k: (0,) * len(shape))

    plane_spec = pl.BlockSpec(
        (None, None, block_y, 1, depth_z), lambda i, k: (k[0], component, 0, 0, 0)
    )
    in_specs = [whole(cur.shape), whole(prev.shape), whole(s.shape), whole(xlo.shape), whole(xhi.shape), plane_spec]
    operands = [cur, prev, s, xlo, xhi, planes]
    halo_shape = jax.ShapeDtypeStruct(xlo.shape, jnp.float32)
    out_shape = [jax.ShapeDtypeStruct(cur.shape, jnp.float32), halo_shape, halo_shape]
    out_specs = [whole(cur.shape), whole(xlo.shape), whole(xlo.shape)]
    aliases = {2: 0}
    if with_image:
        in_specs += [whole(other.shape), whole(img.shape)]
        operands += [other, img]
        out_shape.append(jax.ShapeDtypeStruct(img.shape, jnp.float32))
        out_specs.append(whole(img.shape))
        aliases[8] = 3
    grid_spec = pltpu.PrefetchScalarGridSpec(
        num_scalar_prefetch=1,
        grid=(1,),
        in_specs=in_specs,
        out_specs=tuple(out_specs),
        scratch_shapes=[
            pltpu.VMEM((block_y + 2 * HALO, block_x, depth_z), jnp.float32),
            pltpu.VMEM((2, block_y, block_x, depth_z), jnp.float32),
        ],
    )
    return pl.pallas_call(
        functools.partial(wave_kernel, with_image),
        out_shape=tuple(out_shape),
        grid_spec=grid_spec,
        input_output_aliases=aliases,
        compiler_params=pltpu.CompilerParams(vmem_limit_bytes=48 * 1024 * 1024),
        cost_estimate=pl.CostEstimate(
            flops=60 * cur.size, bytes_accessed=4 * 6 * cur.size, transcendentals=0
        ),
    )(jnp.reshape(moment, (1,)).astype(jnp.int32), *operands)


def point_tables(cell_rows, x_start, cells_wide, depth_y):
    local_x = cell_rows[0] - x_start
    inside = (local_x >= 0) & (local_x < cells_wide)
    rows_y = (cell_rows[1][:, None] == jnp.arange(depth_y, dtype=jnp.int32)[None, :]).astype(
        jnp.float32
    )
    column = local_x * 4 + cell_rows[2]
    places = (column[:, None] == jnp.arange(cells_wide * 4, dtype=jnp.int32)[None, :]) & inside[
        :, None
    ]
    return (rows_y, places.astype(jnp.float32))


def spread_points(tables, amounts):
    rows_y, places = tables
    weighted = places[:, None, :] * jnp.transpose(amounts)[:, :, None]
    return jnp.einsum("ny,nsc->syc", rows_y, weighted, precision=lax.Precision.HIGHEST)


def shards(older_fields, fields_now, velocity, aperture, source_pos, wavelet, receiver_pos, traces):
    slab_count = lax.axis_size("dom")
    depth_y = fields_now.shape[1]
    cells_x = fields_now.shape[2]
    depth_z = fields_now.shape[3]
    block_y = velocity.shape[0]
    steps_total = wavelet.shape[0]
    x_anchor = lax.axis_index("dom") * cells_x
    bricks = velocity.reshape(block_y, slab_count, cells_x, depth_z)
    chosen = jnp.take(bricks, aperture, axis=1)
    arrived = lax.all_to_all(chosen, "dom", split_axis=1, concat_axis=0, tiled=True)
    scaled = courant * arrived.reshape(depth_y, cells_x, depth_z)
    speed_sq = scaled * scaled
    image_zero = jnp.zeros((depth_y, cells_x, depth_z), jnp.float32)
    source_core = point_tables(source_pos, x_anchor, cells_x, depth_y)
    receiver_core = point_tables(receiver_pos, x_anchor, cells_x, depth_y)

    planes = jnp.stack(
        [spread_points(source_core, wavelet), spread_points(receiver_core, traces)], axis=1
    )
    planes = planes.reshape(steps_total, 2, depth_y, cells_x, 4)
    gap = jnp.zeros((steps_total, 2, depth_y, depth_z - 4 * cells_x), jnp.float32)
    tail = planes[:, :, :, :0:-1].reshape(steps_total, 2, depth_y, 4 * (cells_x - 1))
    planes = jnp.concatenate([planes[:, :, :, 0], gap, tail], axis=3)
    planes = planes.reshape(steps_total, 2, depth_y, 1, depth_z)

    def advance(moment, state):
        (prev0, cur0, head0, tail0), (prev1, cur1, head1, tail1), image_acc = state
        low0, high0 = trade_halos(head0, tail0, "dom")
        low1, high1 = trade_halos(head1, tail1, "dom")
        new0, head0, tail0 = wave_call(0, moment, cur0, prev0, speed_sq, low0, high0, planes)
        new1, head1, tail1, image_acc = wave_call(
            1, moment, cur1, prev1, speed_sq, low1, high1, planes, new0, image_acc
        )
        return (cur0, new0, head0, tail0), (cur1, new1, head1, tail1), image_acc

    def pair(index, state):
        return advance(2 * index + 1, advance(2 * index, state))

    def edges(field):
        return (field[:, :HALO], field[:, cells_x - HALO :])

    start = (
        (older_fields[0], fields_now[0]) + edges(fields_now[0]),
        (older_fields[1], fields_now[1]) + edges(fields_now[1]),
        image_zero,
    )
    state = lax.fori_loop(0, steps_total // 2, pair, start)
    if steps_total % 2:
        state = advance(steps_total - 1, state)
    (prev0, cur0, _, _), (prev1, cur1, _, _), image_acc = state
    previous = jnp.stack([prev0, prev1])
    current = jnp.stack([cur0, cur1])
    image_acc = image_acc * (1.0 / steps_total)
    outgoing = image_acc.reshape(depth_y, 1, cells_x, depth_z)
    one_hot = (aperture[None, :] == jnp.arange(slab_count, dtype=jnp.int32)[:, None]).astype(
        jnp.float32
    )
    received = lax.all_to_all(outgoing, "dom", split_axis=0, concat_axis=1, tiled=True)
    summed = jnp.einsum("mj,yjcz->ymcz", one_hot, received, precision=lax.Precision.HIGHEST)
    image_model = summed.reshape(received.shape[0], slab_count * cells_x, received.shape[3])
    return (previous, current, image_model)


def solution(mesh):
    in_specs = (
        P(None, "survey", "dom", None),
        P(None, "survey", "dom", None),
        P("dom", "survey", None),
        P("survey"),
        P(None, "survey"),
        P(None, "survey"),
        P(None, "survey"),
        P(None, "survey"),
    )
    out_specs = (
        P(None, "survey", "dom", None),
        P(None, "survey", "dom", None),
        P("dom", "survey", None),
    )
    return jax.shard_map(shards, mesh=mesh, in_specs=in_specs, out_specs=out_specs, check_vma=False)
```

```python
import functools

import jax
import jax.numpy as jnp
from jax import lax
from jax.experimental import pallas as pl
from jax.experimental.pallas import tpu as pltpu
from jax.sharding import PartitionSpec as P

courant = 0.09
stencil_weights = (8.0 / 5.0, -1.0 / 5.0, 8.0 / 315.0, -1.0 / 560.0)
center_weight = 3.0 * (-205.0 / 72.0)
HALO = 4
ROWS = 64
XOFF = 8


def trade_halos(head, tail, axis):
    count = lax.axis_size(axis)
    ends = count - 1
    low = lax.ppermute(tail, axis, [(i, (i + 1) % count) for i in range(ends)])
    high = lax.ppermute(head, axis, [((i + 1) % count, i) for i in range(ends)])
    return low, high


def wave_kernel(with_image, moment_ref, cur_ref, prev_ref, s_ref, xlo_ref, xhi_ref, inj_ref, *rest):
    if with_image:
        other_ref, img_ref, out_ref, head_ref, tail_ref, imgo_ref, ey_ref, hx_ref = rest
    else:
        out_ref, head_ref, tail_ref, ey_ref, hx_ref = rest
    block_y, block_x, depth_z = cur_ref.shape
    zeros_y = jnp.zeros((HALO, block_x, depth_z), jnp.float32)
    ey_ref[0:HALO] = zeros_y
    ey_ref[HALO + block_y : 2 * HALO + block_y] = zeros_y
    ey_ref[HALO : HALO + block_y] = cur_ref[...]
    hx_ref[0, :, block_x - HALO : block_x, :] = xlo_ref[...]
    hx_ref[1, :, 0:HALO, :] = xhi_ref[...]
    rows = ROWS
    lane = lax.broadcasted_iota(jnp.int32, (rows, block_x, depth_z), 2)
    sub = lax.broadcasted_iota(jnp.int32, (rows, block_x, depth_z), 1)

    def chunk(index, carry):
        y = pl.multiple_of(index * rows, rows)
        ctr = ey_ref[pl.ds(HALO + y, rows)]
        left = hx_ref[0, pl.ds(y, rows)]
        right = hx_ref[1, pl.ds(y, rows)]
        acc = center_weight * ctr
        for m in range(1, HALO + 1):
            ahead = pltpu.roll(jnp.where(sub >= m, ctr, right), block_x - m, 1)
            behind = pltpu.roll(jnp.where(sub < block_x - m, ctr, left), m, 1)
            b = ahead + behind
            b = b + ey_ref[pl.ds(HALO + y + m, rows)] + ey_ref[pl.ds(HALO + y - m, rows)]
            up = jnp.where(lane < depth_z - m, pltpu.roll(ctr, depth_z - m, 2), 0.0)
            down = jnp.where(lane >= m, pltpu.roll(ctr, m, 2), 0.0)
            b = b + up + down
            acc = acc + stencil_weights[m - 1] * b
        spread = jnp.broadcast_to(inj_ref[pl.ds(y, rows)], (rows, block_x, depth_z))
        spread = pltpu.roll(spread, 0, 2, stride=4, stride_axis=1)
        lap = acc + jnp.where(lane < 4, spread, 0.0)
        upd = 2.0 * ctr - prev_ref[pl.ds(y, rows)] + s_ref[pl.ds(y, rows)] * lap
        out_ref[pl.ds(y, rows)] = upd
        head_ref[pl.ds(y, rows)] = upd[:, 0:HALO]
        tail_ref[pl.ds(y, rows)] = upd[:, block_x - HALO : block_x]
        if with_image:
            imgo_ref[pl.ds(y, rows)] = img_ref[pl.ds(y, rows)] + other_ref[pl.ds(y, rows)] * upd
        return carry

    lax.fori_loop(0, block_y // rows, chunk, 0)


def wave_call(component, moment, cur, prev, s, xlo, xhi, planes, other=None, img=None):
    block_y, block_x, depth_z = cur.shape
    with_image = img is not None

    def whole(shape):
        return pl.BlockSpec(shape, lambda i, k: (0,) * len(shape))

    plane_spec = pl.BlockSpec(
        (None, None, block_y, 1, depth_z), lambda i, k: (k[0], component, 0, 0, 0)
    )
    in_specs = [whole(cur.shape), whole(prev.shape), whole(s.shape), whole(xlo.shape), whole(xhi.shape), plane_spec]
    operands = [cur, prev, s, xlo, xhi, planes]
    halo_shape = jax.ShapeDtypeStruct(xlo.shape, jnp.float32)
    out_shape = [jax.ShapeDtypeStruct(cur.shape, jnp.float32), halo_shape, halo_shape]
    out_specs = [whole(cur.shape), whole(xlo.shape), whole(xlo.shape)]
    aliases = {2: 0}
    if with_image:
        in_specs += [whole(other.shape), whole(img.shape)]
        operands += [other, img]
        out_shape.append(jax.ShapeDtypeStruct(img.shape, jnp.float32))
        out_specs.append(whole(img.shape))
        aliases[8] = 3
    grid_spec = pltpu.PrefetchScalarGridSpec(
        num_scalar_prefetch=1,
        grid=(1,),
        in_specs=in_specs,
        out_specs=tuple(out_specs),
        scratch_shapes=[
            pltpu.VMEM((block_y + 2 * HALO, block_x, depth_z), jnp.float32),
            pltpu.VMEM((2, block_y, block_x, depth_z), jnp.float32),
        ],
    )
    return pl.pallas_call(
        functools.partial(wave_kernel, with_image),
        out_shape=tuple(out_shape),
        grid_spec=grid_spec,
        input_output_aliases=aliases,
        compiler_params=pltpu.CompilerParams(vmem_limit_bytes=48 * 1024 * 1024),
        cost_estimate=pl.CostEstimate(
            flops=60 * cur.size, bytes_accessed=4 * 6 * cur.size, transcendentals=0
        ),
    )(jnp.reshape(moment, (1,)).astype(jnp.int32), *operands)


def point_tables(cell_rows, x_start, cells_wide, depth_y):
    local_x = cell_rows[0] - x_start
    inside = (local_x >= 0) & (local_x < cells_wide)
    rows_y = (cell_rows[1][:, None] == jnp.arange(depth_y, dtype=jnp.int32)[None, :]).astype(
        jnp.float32
    )
    column = local_x * 4 + cell_rows[2]
    places = (column[:, None] == jnp.arange(cells_wide * 4, dtype=jnp.int32)[None, :]) & inside[
        :, None
    ]
    return (rows_y, places.astype(jnp.float32))


def spread_points(tables, amounts):
    rows_y, places = tables
    weighted = places[:, None, :] * jnp.transpose(amounts)[:, :, None]
    return jnp.einsum("ny,nsc->syc", rows_y, weighted, precision=lax.Precision.HIGHEST)


def shards(older_fields, fields_now, velocity, aperture, source_pos, wavelet, receiver_pos, traces):
    slab_count = lax.axis_size("dom")
    depth_y = fields_now.shape[1]
    cells_x = fields_now.shape[2]
    depth_z = fields_now.shape[3]
    block_y = velocity.shape[0]
    steps_total = wavelet.shape[0]
    x_anchor = lax.axis_index("dom") * cells_x
    bricks = velocity.reshape(block_y, slab_count, cells_x, depth_z)
    chosen = jnp.take(bricks, aperture, axis=1)
    arrived = lax.all_to_all(chosen, "dom", split_axis=1, concat_axis=0, tiled=True)
    scaled = courant * arrived.reshape(depth_y, cells_x, depth_z)
    speed_sq = scaled * scaled
    image_zero = jnp.zeros((depth_y, cells_x, depth_z), jnp.float32)
    source_core = point_tables(source_pos, x_anchor, cells_x, depth_y)
    receiver_core = point_tables(receiver_pos, x_anchor, cells_x, depth_y)

    planes = jnp.stack(
        [spread_points(source_core, wavelet), spread_points(receiver_core, traces)], axis=1
    )
    planes = planes.reshape(steps_total, 2, depth_y, cells_x, 4)
    gap = jnp.zeros((steps_total, 2, depth_y, depth_z - 4 * cells_x), jnp.float32)
    tail = planes[:, :, :, :0:-1].reshape(steps_total, 2, depth_y, 4 * (cells_x - 1))
    planes = jnp.concatenate([planes[:, :, :, 0], gap, tail], axis=3)
    planes = planes.reshape(steps_total, 2, depth_y, 1, depth_z)

    def advance(moment, state):
        (prev0, cur0, head0, tail0), (prev1, cur1, head1, tail1), image_acc = state
        low0, high0 = trade_halos(head0, tail0, "dom")
        low1, high1 = trade_halos(head1, tail1, "dom")
        new0, head0, tail0 = wave_call(0, moment, cur0, prev0, speed_sq, low0, high0, planes)
        new1, head1, tail1, image_acc = wave_call(
            1, moment, cur1, prev1, speed_sq, low1, high1, planes, new0, image_acc
        )
        return (cur0, new0, head0, tail0), (cur1, new1, head1, tail1), image_acc

    def pair(index, state):
        return advance(2 * index + 1, advance(2 * index, state))

    def edges(field):
        return (field[:, :HALO], field[:, cells_x - HALO :])

    start = (
        (older_fields[0], fields_now[0]) + edges(fields_now[0]),
        (older_fields[1], fields_now[1]) + edges(fields_now[1]),
        image_zero,
    )
    state = lax.fori_loop(0, steps_total // 2, pair, start)
    if steps_total % 2:
        state = advance(steps_total - 1, state)
    (prev0, cur0, _, _), (prev1, cur1, _, _), image_acc = state
    previous = jnp.stack([prev0, prev1])
    current = jnp.stack([cur0, cur1])
    image_acc = image_acc * (1.0 / steps_total)
    outgoing = image_acc.reshape(depth_y, 1, cells_x, depth_z)
    one_hot = (aperture[None, :] == jnp.arange(slab_count, dtype=jnp.int32)[:, None]).astype(
        jnp.float32
    )
    received = lax.all_to_all(outgoing, "dom", split_axis=0, concat_axis=1, tiled=True)
    summed = jnp.einsum("mj,yjcz->ymcz", one_hot, received, precision=lax.Precision.HIGHEST)
    image_model = summed.reshape(received.shape[0], slab_count * cells_x, received.shape[3])
    return (previous, current, image_model)


def solution(mesh):
    in_specs = (
        P(None, "survey", "dom", None),
        P(None, "survey", "dom", None),
        P("dom", "survey", None),
        P("survey"),
        P(None, "survey"),
        P(None, "survey"),
        P(None, "survey"),
        P(None, "survey"),
    )
    out_specs = (
        P(None, "survey", "dom", None),
        P(None, "survey", "dom", None),
        P("dom", "survey", None),
    )
    return jax.shard_map(shards, mesh=mesh, in_specs=in_specs, out_specs=out_specs, check_vma=False)
```

```python
import functools

import jax
import jax.numpy as jnp
from jax import lax
from jax.experimental import pallas as pl
from jax.experimental.pallas import tpu as pltpu
from jax.sharding import PartitionSpec as P

courant = 0.09
stencil_weights = (8.0 / 5.0, -1.0 / 5.0, 8.0 / 315.0, -1.0 / 560.0)
center_weight = 3.0 * (-205.0 / 72.0)
HALO = 4
ROWS = 128
XOFF = 8


def trade_halos(head, tail, axis):
    count = lax.axis_size(axis)
    ends = count - 1
    low = lax.ppermute(tail, axis, [(i, (i + 1) % count) for i in range(ends)])
    high = lax.ppermute(head, axis, [((i + 1) % count, i) for i in range(ends)])
    return low, high


def wave_kernel(with_image, moment_ref, cur_ref, prev_ref, s_ref, xlo_ref, xhi_ref, inj_ref, *rest):
    if with_image:
        other_ref, img_ref, out_ref, head_ref, tail_ref, imgo_ref, ey_ref, hx_ref = rest
    else:
        out_ref, head_ref, tail_ref, ey_ref, hx_ref = rest
    block_y, block_x, depth_z = cur_ref.shape
    zeros_y = jnp.zeros((HALO, block_x, depth_z), jnp.float32)
    ey_ref[0:HALO] = zeros_y
    ey_ref[HALO + block_y : 2 * HALO + block_y] = zeros_y
    ey_ref[HALO : HALO + block_y] = cur_ref[...]
    hx_ref[0, :, block_x - HALO : block_x, :] = xlo_ref[...]
    hx_ref[1, :, 0:HALO, :] = xhi_ref[...]
    rows = ROWS
    lane = lax.broadcasted_iota(jnp.int32, (rows, block_x, depth_z), 2)
    sub = lax.broadcasted_iota(jnp.int32, (rows, block_x, depth_z), 1)

    def chunk(index, carry):
        y = pl.multiple_of(index * rows, rows)
        ctr = ey_ref[pl.ds(HALO + y, rows)]
        left = hx_ref[0, pl.ds(y, rows)]
        right = hx_ref[1, pl.ds(y, rows)]
        acc = center_weight * ctr
        for m in range(1, HALO + 1):
            ahead = pltpu.roll(jnp.where(sub >= m, ctr, right), block_x - m, 1)
            behind = pltpu.roll(jnp.where(sub < block_x - m, ctr, left), m, 1)
            b = ahead + behind
            b = b + ey_ref[pl.ds(HALO + y + m, rows)] + ey_ref[pl.ds(HALO + y - m, rows)]
            up = jnp.where(lane < depth_z - m, pltpu.roll(ctr, depth_z - m, 2), 0.0)
            down = jnp.where(lane >= m, pltpu.roll(ctr, m, 2), 0.0)
            b = b + up + down
            acc = acc + stencil_weights[m - 1] * b
        spread = jnp.broadcast_to(inj_ref[pl.ds(y, rows)], (rows, block_x, depth_z))
        spread = pltpu.roll(spread, 0, 2, stride=4, stride_axis=1)
        lap = acc + jnp.where(lane < 4, spread, 0.0)
        upd = 2.0 * ctr - prev_ref[pl.ds(y, rows)] + s_ref[pl.ds(y, rows)] * lap
        out_ref[pl.ds(y, rows)] = upd
        head_ref[pl.ds(y, rows)] = upd[:, 0:HALO]
        tail_ref[pl.ds(y, rows)] = upd[:, block_x - HALO : block_x]
        if with_image:
            imgo_ref[pl.ds(y, rows)] = img_ref[pl.ds(y, rows)] + other_ref[pl.ds(y, rows)] * upd
        return carry

    lax.fori_loop(0, block_y // rows, chunk, 0)


def wave_call(component, moment, cur, prev, s, xlo, xhi, planes, other=None, img=None):
    block_y, block_x, depth_z = cur.shape
    with_image = img is not None

    def whole(shape):
        return pl.BlockSpec(shape, lambda i, k: (0,) * len(shape))

    plane_spec = pl.BlockSpec(
        (None, None, block_y, 1, depth_z), lambda i, k: (k[0], component, 0, 0, 0)
    )
    in_specs = [whole(cur.shape), whole(prev.shape), whole(s.shape), whole(xlo.shape), whole(xhi.shape), plane_spec]
    operands = [cur, prev, s, xlo, xhi, planes]
    halo_shape = jax.ShapeDtypeStruct(xlo.shape, jnp.float32)
    out_shape = [jax.ShapeDtypeStruct(cur.shape, jnp.float32), halo_shape, halo_shape]
    out_specs = [whole(cur.shape), whole(xlo.shape), whole(xlo.shape)]
    aliases = {2: 0}
    if with_image:
        in_specs += [whole(other.shape), whole(img.shape)]
        operands += [other, img]
        out_shape.append(jax.ShapeDtypeStruct(img.shape, jnp.float32))
        out_specs.append(whole(img.shape))
        aliases[8] = 3
    grid_spec = pltpu.PrefetchScalarGridSpec(
        num_scalar_prefetch=1,
        grid=(1,),
        in_specs=in_specs,
        out_specs=tuple(out_specs),
        scratch_shapes=[
            pltpu.VMEM((block_y + 2 * HALO, block_x, depth_z), jnp.float32),
            pltpu.VMEM((2, block_y, block_x, depth_z), jnp.float32),
        ],
    )
    return pl.pallas_call(
        functools.partial(wave_kernel, with_image),
        out_shape=tuple(out_shape),
        grid_spec=grid_spec,
        input_output_aliases=aliases,
        compiler_params=pltpu.CompilerParams(vmem_limit_bytes=48 * 1024 * 1024),
        cost_estimate=pl.CostEstimate(
            flops=60 * cur.size, bytes_accessed=4 * 6 * cur.size, transcendentals=0
        ),
    )(jnp.reshape(moment, (1,)).astype(jnp.int32), *operands)


def point_tables(cell_rows, x_start, cells_wide, depth_y):
    local_x = cell_rows[0] - x_start
    inside = (local_x >= 0) & (local_x < cells_wide)
    rows_y = (cell_rows[1][:, None] == jnp.arange(depth_y, dtype=jnp.int32)[None, :]).astype(
        jnp.float32
    )
    column = local_x * 4 + cell_rows[2]
    places = (column[:, None] == jnp.arange(cells_wide * 4, dtype=jnp.int32)[None, :]) & inside[
        :, None
    ]
    return (rows_y, places.astype(jnp.float32))


def spread_points(tables, amounts):
    rows_y, places = tables
    weighted = places[:, None, :] * jnp.transpose(amounts)[:, :, None]
    return jnp.einsum("ny,nsc->syc", rows_y, weighted, precision=lax.Precision.HIGHEST)


def shards(older_fields, fields_now, velocity, aperture, source_pos, wavelet, receiver_pos, traces):
    slab_count = lax.axis_size("dom")
    depth_y = fields_now.shape[1]
    cells_x = fields_now.shape[2]
    depth_z = fields_now.shape[3]
    block_y = velocity.shape[0]
    steps_total = wavelet.shape[0]
    x_anchor = lax.axis_index("dom") * cells_x
    bricks = velocity.reshape(block_y, slab_count, cells_x, depth_z)
    chosen = jnp.take(bricks, aperture, axis=1)
    arrived = lax.all_to_all(chosen, "dom", split_axis=1, concat_axis=0, tiled=True)
    scaled = courant * arrived.reshape(depth_y, cells_x, depth_z)
    speed_sq = scaled * scaled
    image_zero = jnp.zeros((depth_y, cells_x, depth_z), jnp.float32)
    source_core = point_tables(source_pos, x_anchor, cells_x, depth_y)
    receiver_core = point_tables(receiver_pos, x_anchor, cells_x, depth_y)

    planes = jnp.stack(
        [spread_points(source_core, wavelet), spread_points(receiver_core, traces)], axis=1
    )
    planes = planes.reshape(steps_total, 2, depth_y, cells_x, 4)
    gap = jnp.zeros((steps_total, 2, depth_y, depth_z - 4 * cells_x), jnp.float32)
    tail = planes[:, :, :, :0:-1].reshape(steps_total, 2, depth_y, 4 * (cells_x - 1))
    planes = jnp.concatenate([planes[:, :, :, 0], gap, tail], axis=3)
    planes = planes.reshape(steps_total, 2, depth_y, 1, depth_z)

    def advance(moment, state):
        (prev0, cur0, head0, tail0), (prev1, cur1, head1, tail1), image_acc = state
        low0, high0 = trade_halos(head0, tail0, "dom")
        low1, high1 = trade_halos(head1, tail1, "dom")
        new0, head0, tail0 = wave_call(0, moment, cur0, prev0, speed_sq, low0, high0, planes)
        new1, head1, tail1, image_acc = wave_call(
            1, moment, cur1, prev1, speed_sq, low1, high1, planes, new0, image_acc
        )
        return (cur0, new0, head0, tail0), (cur1, new1, head1, tail1), image_acc

    def pair(index, state):
        return advance(2 * index + 1, advance(2 * index, state))

    def edges(field):
        return (field[:, :HALO], field[:, cells_x - HALO :])

    start = (
        (older_fields[0], fields_now[0]) + edges(fields_now[0]),
        (older_fields[1], fields_now[1]) + edges(fields_now[1]),
        image_zero,
    )
    state = lax.fori_loop(0, steps_total // 2, pair, start)
    if steps_total % 2:
        state = advance(steps_total - 1, state)
    (prev0, cur0, _, _), (prev1, cur1, _, _), image_acc = state
    previous = jnp.stack([prev0, prev1])
    current = jnp.stack([cur0, cur1])
    image_acc = image_acc * (1.0 / steps_total)
    outgoing = image_acc.reshape(depth_y, 1, cells_x, depth_z)
    one_hot = (aperture[None, :] == jnp.arange(slab_count, dtype=jnp.int32)[:, None]).astype(
        jnp.float32
    )
    received = lax.all_to_all(outgoing, "dom", split_axis=0, concat_axis=1, tiled=True)
    summed = jnp.einsum("mj,yjcz->ymcz", one_hot, received, precision=lax.Precision.HIGHEST)
    image_model = summed.reshape(received.shape[0], slab_count * cells_x, received.shape[3])
    return (previous, current, image_model)


def solution(mesh):
    in_specs = (
        P(None, "survey", "dom", None),
        P(None, "survey", "dom", None),
        P("dom", "survey", None),
        P("survey"),
        P(None, "survey"),
        P(None, "survey"),
        P(None, "survey"),
        P(None, "survey"),
    )
    out_specs = (
        P(None, "survey", "dom", None),
        P(None, "survey", "dom", None),
        P("dom", "survey", None),
    )
    return jax.shard_map(shards, mesh=mesh, in_specs=in_specs, out_specs=out_specs, check_vma=False)
```

```python
import functools

import jax
import jax.numpy as jnp
from jax import lax
from jax.experimental import pallas as pl
from jax.experimental.pallas import tpu as pltpu
from jax.sharding import PartitionSpec as P

courant = 0.09
stencil_weights = (8.0 / 5.0, -1.0 / 5.0, 8.0 / 315.0, -1.0 / 560.0)
center_weight = 3.0 * (-205.0 / 72.0)
HALO = 4
ROWS = 128
XOFF = 8


def trade_halos(head, tail, axis):
    count = lax.axis_size(axis)
    ends = count - 1
    low = lax.ppermute(tail, axis, [(i, (i + 1) % count) for i in range(ends)])
    high = lax.ppermute(head, axis, [((i + 1) % count, i) for i in range(ends)])
    return low, high


def wave_kernel(with_image, moment_ref, cur_ref, prev_ref, s_ref, xlo_ref, xhi_ref, inj_ref, *rest):
    if with_image:
        other_ref, img_ref, out_ref, head_ref, tail_ref, imgo_ref, ey_ref, hx_ref = rest
    else:
        out_ref, head_ref, tail_ref, ey_ref, hx_ref = rest
    block_y, block_x, depth_z = cur_ref.shape
    zeros_y = jnp.zeros((HALO, block_x, depth_z), jnp.float32)
    ey_ref[0:HALO] = zeros_y
    ey_ref[HALO + block_y : 2 * HALO + block_y] = zeros_y
    ey_ref[HALO : HALO + block_y] = cur_ref[...]
    hx_ref[0, :, block_x - HALO : block_x, :] = xlo_ref[...]
    hx_ref[1, :, 0:HALO, :] = xhi_ref[...]
    rows = ROWS
    lane = lax.broadcasted_iota(jnp.int32, (rows, block_x, depth_z), 2)
    sub = lax.broadcasted_iota(jnp.int32, (rows, block_x, depth_z), 1)

    def chunk(index, carry):
        y = pl.multiple_of(index * rows, rows)
        ctr = ey_ref[pl.ds(HALO + y, rows)]
        left = hx_ref[0, pl.ds(y, rows)]
        right = hx_ref[1, pl.ds(y, rows)]
        acc = center_weight * ctr
        for m in range(1, HALO + 1):
            ahead = pltpu.roll(jnp.where(sub >= m, ctr, right), block_x - m, 1)
            behind = pltpu.roll(jnp.where(sub < block_x - m, ctr, left), m, 1)
            b = ahead + behind
            b = b + ey_ref[pl.ds(HALO + y + m, rows)] + ey_ref[pl.ds(HALO + y - m, rows)]
            up = jnp.where(lane < depth_z - m, pltpu.roll(ctr, depth_z - m, 2), 0.0)
            down = jnp.where(lane >= m, pltpu.roll(ctr, m, 2), 0.0)
            b = b + up + down
            acc = acc + stencil_weights[m - 1] * b
        spread = jnp.broadcast_to(inj_ref[pl.ds(y, rows)], (rows, block_x, depth_z))
        spread = pltpu.roll(spread, 0, 2, stride=4, stride_axis=1)
        lap = acc + jnp.where(lane < 4, spread, 0.0)
        upd = 2.0 * ctr - prev_ref[pl.ds(y, rows)] + s_ref[pl.ds(y, rows)] * lap
        out_ref[pl.ds(y, rows)] = upd
        head_ref[pl.ds(y, rows)] = upd[:, 0:HALO]
        tail_ref[pl.ds(y, rows)] = upd[:, block_x - HALO : block_x]
        if with_image:
            imgo_ref[pl.ds(y, rows)] = img_ref[pl.ds(y, rows)] + other_ref[pl.ds(y, rows)] * upd
        return carry

    lax.fori_loop(0, block_y // rows, chunk, 0)


def wave_call(component, moment, cur, prev, s, xlo, xhi, planes, other=None, img=None):
    block_y, block_x, depth_z = cur.shape
    with_image = img is not None

    def whole(shape):
        return pl.BlockSpec(shape, lambda i, k: (0,) * len(shape))

    plane_spec = pl.BlockSpec(
        (None, None, block_y, 1, depth_z), lambda i, k: (k[0], component, 0, 0, 0)
    )
    in_specs = [whole(cur.shape), whole(prev.shape), whole(s.shape), whole(xlo.shape), whole(xhi.shape), plane_spec]
    operands = [cur, prev, s, xlo, xhi, planes]
    halo_shape = jax.ShapeDtypeStruct(xlo.shape, jnp.float32)
    out_shape = [jax.ShapeDtypeStruct(cur.shape, jnp.float32), halo_shape, halo_shape]
    out_specs = [whole(cur.shape), whole(xlo.shape), whole(xlo.shape)]
    aliases = {2: 0}
    if with_image:
        in_specs += [whole(other.shape), whole(img.shape)]
        operands += [other, img]
        out_shape.append(jax.ShapeDtypeStruct(img.shape, jnp.float32))
        out_specs.append(whole(img.shape))
        aliases[8] = 3
    grid_spec = pltpu.PrefetchScalarGridSpec(
        num_scalar_prefetch=1,
        grid=(1,),
        in_specs=in_specs,
        out_specs=tuple(out_specs),
        scratch_shapes=[
            pltpu.VMEM((block_y + 2 * HALO, block_x, depth_z), jnp.float32),
            pltpu.VMEM((2, block_y, block_x, depth_z), jnp.float32),
        ],
    )
    return pl.pallas_call(
        functools.partial(wave_kernel, with_image),
        out_shape=tuple(out_shape),
        grid_spec=grid_spec,
        input_output_aliases=aliases,
        compiler_params=pltpu.CompilerParams(vmem_limit_bytes=48 * 1024 * 1024),
        cost_estimate=pl.CostEstimate(
            flops=60 * cur.size, bytes_accessed=4 * 6 * cur.size, transcendentals=0
        ),
    )(jnp.reshape(moment, (1,)).astype(jnp.int32), *operands)


def point_tables(cell_rows, x_start, cells_wide, depth_y):
    local_x = cell_rows[0] - x_start
    inside = (local_x >= 0) & (local_x < cells_wide)
    rows_y = (cell_rows[1][:, None] == jnp.arange(depth_y, dtype=jnp.int32)[None, :]).astype(
        jnp.float32
    )
    column = local_x * 4 + cell_rows[2]
    places = (column[:, None] == jnp.arange(cells_wide * 4, dtype=jnp.int32)[None, :]) & inside[
        :, None
    ]
    return (rows_y, places.astype(jnp.float32))


def spread_points(tables, amounts):
    rows_y, places = tables
    rows_y = rows_y.astype(jnp.bfloat16)
    rest = jnp.transpose(amounts)
    total = None
    for _ in range(3):
        piece = rest.astype(jnp.bfloat16)
        rest = rest - piece.astype(jnp.float32)
        weighted = places.astype(jnp.bfloat16)[:, None, :] * piece[:, :, None]
        term = jnp.einsum("ny,nsc->syc", rows_y, weighted, preferred_element_type=jnp.float32)
        total = term if total is None else total + term
    return total


def shards(older_fields, fields_now, velocity, aperture, source_pos, wavelet, receiver_pos, traces):
    slab_count = lax.axis_size("dom")
    depth_y = fields_now.shape[1]
    cells_x = fields_now.shape[2]
    depth_z = fields_now.shape[3]
    block_y = velocity.shape[0]
    steps_total = wavelet.shape[0]
    x_anchor = lax.axis_index("dom") * cells_x
    bricks = velocity.reshape(block_y, slab_count, cells_x, depth_z)
    chosen = jnp.take(bricks, aperture, axis=1)
    arrived = lax.all_to_all(chosen, "dom", split_axis=1, concat_axis=0, tiled=True)
    scaled = courant * arrived.reshape(depth_y, cells_x, depth_z)
    speed_sq = scaled * scaled
    image_zero = jnp.zeros((depth_y, cells_x, depth_z), jnp.float32)
    source_core = point_tables(source_pos, x_anchor, cells_x, depth_y)
    receiver_core = point_tables(receiver_pos, x_anchor, cells_x, depth_y)

    planes = jnp.stack(
        [spread_points(source_core, wavelet), spread_points(receiver_core, traces)], axis=1
    )
    planes = planes.reshape(steps_total, 2, depth_y, cells_x, 4)
    gap = jnp.zeros((steps_total, 2, depth_y, depth_z - 4 * cells_x), jnp.float32)
    tail = planes[:, :, :, :0:-1].reshape(steps_total, 2, depth_y, 4 * (cells_x - 1))
    planes = jnp.concatenate([planes[:, :, :, 0], gap, tail], axis=3)
    planes = planes.reshape(steps_total, 2, depth_y, 1, depth_z)

    def advance(moment, state):
        (prev0, cur0, head0, tail0), (prev1, cur1, head1, tail1), image_acc = state
        low0, high0 = trade_halos(head0, tail0, "dom")
        low1, high1 = trade_halos(head1, tail1, "dom")
        new0, head0, tail0 = wave_call(0, moment, cur0, prev0, speed_sq, low0, high0, planes)
        new1, head1, tail1, image_acc = wave_call(
            1, moment, cur1, prev1, speed_sq, low1, high1, planes, new0, image_acc
        )
        return (cur0, new0, head0, tail0), (cur1, new1, head1, tail1), image_acc

    def pair(index, state):
        return advance(2 * index + 1, advance(2 * index, state))

    def edges(field):
        return (field[:, :HALO], field[:, cells_x - HALO :])

    start = (
        (older_fields[0], fields_now[0]) + edges(fields_now[0]),
        (older_fields[1], fields_now[1]) + edges(fields_now[1]),
        image_zero,
    )
    state = lax.fori_loop(0, steps_total // 2, pair, start)
    if steps_total % 2:
        state = advance(steps_total - 1, state)
    (prev0, cur0, _, _), (prev1, cur1, _, _), image_acc = state
    previous = jnp.stack([prev0, prev1])
    current = jnp.stack([cur0, cur1])
    image_acc = image_acc * (1.0 / steps_total)
    outgoing = image_acc.reshape(depth_y, 1, cells_x, depth_z)
    one_hot = (aperture[None, :] == jnp.arange(slab_count, dtype=jnp.int32)[:, None]).astype(
        jnp.float32
    )
    received = lax.all_to_all(outgoing, "dom", split_axis=0, concat_axis=1, tiled=True)
    summed = jnp.einsum("mj,yjcz->ymcz", one_hot, received, precision=lax.Precision.HIGHEST)
    image_model = summed.reshape(received.shape[0], slab_count * cells_x, received.shape[3])
    return (previous, current, image_model)


def solution(mesh):
    in_specs = (
        P(None, "survey", "dom", None),
        P(None, "survey", "dom", None),
        P("dom", "survey", None),
        P("survey"),
        P(None, "survey"),
        P(None, "survey"),
        P(None, "survey"),
        P(None, "survey"),
    )
    out_specs = (
        P(None, "survey", "dom", None),
        P(None, "survey", "dom", None),
        P("dom", "survey", None),
    )
    return jax.shard_map(shards, mesh=mesh, in_specs=in_specs, out_specs=out_specs, check_vma=False)
```

```python
import functools

import jax
import jax.numpy as jnp
from jax import lax
from jax.experimental import pallas as pl
from jax.experimental.pallas import tpu as pltpu
from jax.sharding import PartitionSpec as P

courant = 0.09
stencil_weights = (8.0 / 5.0, -1.0 / 5.0, 8.0 / 315.0, -1.0 / 560.0)
center_weight = 3.0 * (-205.0 / 72.0)
HALO = 4
ROWS = 128
TRIP = 4
XOFF = 8


def trade_halos(head, tail, axis):
    count = lax.axis_size(axis)
    ends = count - 1
    low = lax.ppermute(tail, axis, [(i, (i + 1) % count) for i in range(ends)])
    high = lax.ppermute(head, axis, [((i + 1) % count, i) for i in range(ends)])
    return low, high


def wave_kernel(with_image, moment_ref, cur_ref, prev_ref, s_ref, xlo_ref, xhi_ref, inj_ref, *rest):
    if with_image:
        other_ref, img_ref, out_ref, head_ref, tail_ref, imgo_ref, ey_ref, hx_ref = rest
    else:
        out_ref, head_ref, tail_ref, ey_ref, hx_ref = rest
    block_y, block_x, depth_z = cur_ref.shape
    zeros_y = jnp.zeros((HALO, block_x, depth_z), jnp.float32)
    ey_ref[0:HALO] = zeros_y
    ey_ref[HALO + block_y : 2 * HALO + block_y] = zeros_y
    ey_ref[HALO : HALO + block_y] = cur_ref[...]
    hx_ref[0, :, block_x - HALO : block_x, :] = xlo_ref[...]
    hx_ref[1, :, 0:HALO, :] = xhi_ref[...]
    rows = ROWS
    lane = lax.broadcasted_iota(jnp.int32, (rows, block_x, depth_z), 2)
    sub = lax.broadcasted_iota(jnp.int32, (rows, block_x, depth_z), 1)

    def chunk(index, carry):
        y = pl.multiple_of(index * rows, rows)
        ctr = ey_ref[pl.ds(HALO + y, rows)]
        left = hx_ref[0, pl.ds(y, rows)]
        right = hx_ref[1, pl.ds(y, rows)]
        acc = center_weight * ctr
        for m in range(1, HALO + 1):
            ahead = pltpu.roll(jnp.where(sub >= m, ctr, right), block_x - m, 1)
            behind = pltpu.roll(jnp.where(sub < block_x - m, ctr, left), m, 1)
            b = ahead + behind
            b = b + ey_ref[pl.ds(HALO + y + m, rows)] + ey_ref[pl.ds(HALO + y - m, rows)]
            up = jnp.where(lane < depth_z - m, pltpu.roll(ctr, depth_z - m, 2), 0.0)
            down = jnp.where(lane >= m, pltpu.roll(ctr, m, 2), 0.0)
            b = b + up + down
            acc = acc + stencil_weights[m - 1] * b
        spread = jnp.broadcast_to(inj_ref[pl.ds(y, rows)], (rows, block_x, depth_z))
        spread = pltpu.roll(spread, 0, 2, stride=4, stride_axis=1)
        lap = acc + jnp.where(lane < 4, spread, 0.0)
        upd = 2.0 * ctr - prev_ref[pl.ds(y, rows)] + s_ref[pl.ds(y, rows)] * lap
        out_ref[pl.ds(y, rows)] = upd
        head_ref[pl.ds(y, rows)] = upd[:, 0:HALO]
        tail_ref[pl.ds(y, rows)] = upd[:, block_x - HALO : block_x]
        if with_image:
            imgo_ref[pl.ds(y, rows)] = img_ref[pl.ds(y, rows)] + other_ref[pl.ds(y, rows)] * upd
        return carry

    lax.fori_loop(0, block_y // rows, chunk, 0)


def wave_call(component, moment, cur, prev, s, xlo, xhi, planes, other=None, img=None):
    block_y, block_x, depth_z = cur.shape
    with_image = img is not None

    def whole(shape):
        return pl.BlockSpec(shape, lambda i, k: (0,) * len(shape))

    plane_spec = pl.BlockSpec(
        (None, None, block_y, 1, depth_z), lambda i, k: (k[0], component, 0, 0, 0)
    )
    in_specs = [whole(cur.shape), whole(prev.shape), whole(s.shape), whole(xlo.shape), whole(xhi.shape), plane_spec]
    operands = [cur, prev, s, xlo, xhi, planes]
    halo_shape = jax.ShapeDtypeStruct(xlo.shape, jnp.float32)
    out_shape = [jax.ShapeDtypeStruct(cur.shape, jnp.float32), halo_shape, halo_shape]
    out_specs = [whole(cur.shape), whole(xlo.shape), whole(xlo.shape)]
    aliases = {2: 0}
    if with_image:
        in_specs += [whole(other.shape), whole(img.shape)]
        operands += [other, img]
        out_shape.append(jax.ShapeDtypeStruct(img.shape, jnp.float32))
        out_specs.append(whole(img.shape))
        aliases[8] = 3
    grid_spec = pltpu.PrefetchScalarGridSpec(
        num_scalar_prefetch=1,
        grid=(1,),
        in_specs=in_specs,
        out_specs=tuple(out_specs),
        scratch_shapes=[
            pltpu.VMEM((block_y + 2 * HALO, block_x, depth_z), jnp.float32),
            pltpu.VMEM((2, block_y, block_x, depth_z), jnp.float32),
        ],
    )
    return pl.pallas_call(
        functools.partial(wave_kernel, with_image),
        out_shape=tuple(out_shape),
        grid_spec=grid_spec,
        input_output_aliases=aliases,
        compiler_params=pltpu.CompilerParams(vmem_limit_bytes=48 * 1024 * 1024),
        cost_estimate=pl.CostEstimate(
            flops=60 * cur.size, bytes_accessed=4 * 6 * cur.size, transcendentals=0
        ),
    )(jnp.reshape(moment, (1,)).astype(jnp.int32), *operands)


def point_tables(cell_rows, x_start, cells_wide, depth_y):
    local_x = cell_rows[0] - x_start
    inside = (local_x >= 0) & (local_x < cells_wide)
    rows_y = (cell_rows[1][:, None] == jnp.arange(depth_y, dtype=jnp.int32)[None, :]).astype(
        jnp.float32
    )
    column = local_x * 4 + cell_rows[2]
    places = (column[:, None] == jnp.arange(cells_wide * 4, dtype=jnp.int32)[None, :]) & inside[
        :, None
    ]
    return (rows_y, places.astype(jnp.float32))


def spread_points(tables, amounts):
    rows_y, places = tables
    weighted = places[:, None, :] * jnp.transpose(amounts)[:, :, None]
    return jnp.einsum("ny,nsc->syc", rows_y, weighted, precision=lax.Precision.HIGHEST)


def shards(older_fields, fields_now, velocity, aperture, source_pos, wavelet, receiver_pos, traces):
    slab_count = lax.axis_size("dom")
    depth_y = fields_now.shape[1]
    cells_x = fields_now.shape[2]
    depth_z = fields_now.shape[3]
    block_y = velocity.shape[0]
    steps_total = wavelet.shape[0]
    x_anchor = lax.axis_index("dom") * cells_x
    bricks = velocity.reshape(block_y, slab_count, cells_x, depth_z)
    chosen = jnp.take(bricks, aperture, axis=1)
    arrived = lax.all_to_all(chosen, "dom", split_axis=1, concat_axis=0, tiled=True)
    scaled = courant * arrived.reshape(depth_y, cells_x, depth_z)
    speed_sq = scaled * scaled
    image_zero = jnp.zeros((depth_y, cells_x, depth_z), jnp.float32)
    source_core = point_tables(source_pos, x_anchor, cells_x, depth_y)
    receiver_core = point_tables(receiver_pos, x_anchor, cells_x, depth_y)

    planes = jnp.stack(
        [spread_points(source_core, wavelet), spread_points(receiver_core, traces)], axis=1
    )
    planes = planes.reshape(steps_total, 2, depth_y, cells_x, 4)
    gap = jnp.zeros((steps_total, 2, depth_y, depth_z - 4 * cells_x), jnp.float32)
    tail = planes[:, :, :, :0:-1].reshape(steps_total, 2, depth_y, 4 * (cells_x - 1))
    planes = jnp.concatenate([planes[:, :, :, 0], gap, tail], axis=3)
    planes = planes.reshape(steps_total, 2, depth_y, 1, depth_z)

    def advance(moment, state):
        (prev0, cur0, head0, tail0), (prev1, cur1, head1, tail1), image_acc = state
        low0, high0 = trade_halos(head0, tail0, "dom")
        low1, high1 = trade_halos(head1, tail1, "dom")
        new0, head0, tail0 = wave_call(0, moment, cur0, prev0, speed_sq, low0, high0, planes)
        new1, head1, tail1, image_acc = wave_call(
            1, moment, cur1, prev1, speed_sq, low1, high1, planes, new0, image_acc
        )
        return (cur0, new0, head0, tail0), (cur1, new1, head1, tail1), image_acc

    def pair(index, state):
        for offset in range(TRIP):
            state = advance(TRIP * index + offset, state)
        return state

    def edges(field):
        return (field[:, :HALO], field[:, cells_x - HALO :])

    start = (
        (older_fields[0], fields_now[0]) + edges(fields_now[0]),
        (older_fields[1], fields_now[1]) + edges(fields_now[1]),
        image_zero,
    )
    state = lax.fori_loop(0, steps_total // TRIP, pair, start)
    for moment in range(steps_total - steps_total % TRIP, steps_total):
        state = advance(moment, state)
    (prev0, cur0, _, _), (prev1, cur1, _, _), image_acc = state
    previous = jnp.stack([prev0, prev1])
    current = jnp.stack([cur0, cur1])
    image_acc = image_acc * (1.0 / steps_total)
    outgoing = image_acc.reshape(depth_y, 1, cells_x, depth_z)
    one_hot = (aperture[None, :] == jnp.arange(slab_count, dtype=jnp.int32)[:, None]).astype(
        jnp.float32
    )
    received = lax.all_to_all(outgoing, "dom", split_axis=0, concat_axis=1, tiled=True)
    summed = jnp.einsum("mj,yjcz->ymcz", one_hot, received, precision=lax.Precision.HIGHEST)
    image_model = summed.reshape(received.shape[0], slab_count * cells_x, received.shape[3])
    return (previous, current, image_model)


def solution(mesh):
    in_specs = (
        P(None, "survey", "dom", None),
        P(None, "survey", "dom", None),
        P("dom", "survey", None),
        P("survey"),
        P(None, "survey"),
        P(None, "survey"),
        P(None, "survey"),
        P(None, "survey"),
    )
    out_specs = (
        P(None, "survey", "dom", None),
        P(None, "survey", "dom", None),
        P("dom", "survey", None),
    )
    return jax.shard_map(shards, mesh=mesh, in_specs=in_specs, out_specs=out_specs, check_vma=False)
```

```python
import functools

import jax
import jax.numpy as jnp
from jax import lax
from jax.experimental import pallas as pl
from jax.experimental.pallas import tpu as pltpu
from jax.sharding import PartitionSpec as P

courant = 0.09
stencil_weights = (8.0 / 5.0, -1.0 / 5.0, 8.0 / 315.0, -1.0 / 560.0)
center_weight = 3.0 * (-205.0 / 72.0)
HALO = 4
TRIP = 4


def trade_halos(head, tail, axis):
    count = lax.axis_size(axis)
    ends = count - 1
    low = lax.ppermute(tail, axis, [(i, (i + 1) % count) for i in range(ends)])
    high = lax.ppermute(head, axis, [((i + 1) % count, i) for i in range(ends)])
    return low, high


def wave_kernel(with_image, moment_ref, cur_ref, prev_ref, s_ref, xlo_ref, xhi_ref, inj_ref, *rest):
    if with_image:
        other_ref, img_ref, out_ref, head_ref, tail_ref, imgo_ref, ey_ref, hx_ref = rest
    else:
        out_ref, head_ref, tail_ref, ey_ref, hx_ref = rest
    block_y, block_x, depth_z = cur_ref.shape
    hx_ref[0, :, block_x - HALO : block_x, :] = xlo_ref[...]
    hx_ref[1, :, 0:HALO, :] = xhi_ref[...]
    rows = block_y
    lane = lax.broadcasted_iota(jnp.int32, (rows, block_x, depth_z), 2)
    sub = lax.broadcasted_iota(jnp.int32, (rows, block_x, depth_z), 1)

    def chunk(index, carry):
        y = pl.multiple_of(index * rows, rows)
        ctr = cur_ref[...]
        left = hx_ref[0, pl.ds(y, rows)]
        right = hx_ref[1, pl.ds(y, rows)]
        acc = center_weight * ctr
        for m in range(1, HALO + 1):
            ahead = pltpu.roll(jnp.where(sub >= m, ctr, right), block_x - m, 1)
            behind = pltpu.roll(jnp.where(sub < block_x - m, ctr, left), m, 1)
            b = ahead + behind
            zeros_m = jnp.zeros((m, block_x, depth_z), jnp.float32)
            b = b + jnp.concatenate([ctr[m:], zeros_m], 0) + jnp.concatenate([zeros_m, ctr[:-m]], 0)
            up = jnp.where(lane < depth_z - m, pltpu.roll(ctr, depth_z - m, 2), 0.0)
            down = jnp.where(lane >= m, pltpu.roll(ctr, m, 2), 0.0)
            b = b + up + down
            acc = acc + stencil_weights[m - 1] * b
        spread = jnp.broadcast_to(inj_ref[pl.ds(y, rows)], (rows, block_x, depth_z))
        spread = pltpu.roll(spread, 0, 2, stride=4, stride_axis=1)
        lap = acc + jnp.where(lane < 4, spread, 0.0)
        upd = 2.0 * ctr - prev_ref[pl.ds(y, rows)] + s_ref[pl.ds(y, rows)] * lap
        out_ref[pl.ds(y, rows)] = upd
        head_ref[pl.ds(y, rows)] = upd[:, 0:HALO]
        tail_ref[pl.ds(y, rows)] = upd[:, block_x - HALO : block_x]
        if with_image:
            imgo_ref[pl.ds(y, rows)] = img_ref[pl.ds(y, rows)] + other_ref[pl.ds(y, rows)] * upd
        return carry

    lax.fori_loop(0, block_y // rows, chunk, 0)


def wave_call(component, moment, cur, prev, s, xlo, xhi, planes, other=None, img=None):
    block_y, block_x, depth_z = cur.shape
    with_image = img is not None

    def whole(shape):
        return pl.BlockSpec(shape, lambda i, k: (0,) * len(shape))

    plane_spec = pl.BlockSpec(
        (None, None, block_y, 1, depth_z), lambda i, k: (k[0], component, 0, 0, 0)
    )
    in_specs = [whole(cur.shape), whole(prev.shape), whole(s.shape), whole(xlo.shape), whole(xhi.shape), plane_spec]
    operands = [cur, prev, s, xlo, xhi, planes]
    halo_shape = jax.ShapeDtypeStruct(xlo.shape, jnp.float32)
    out_shape = [jax.ShapeDtypeStruct(cur.shape, jnp.float32), halo_shape, halo_shape]
    out_specs = [whole(cur.shape), whole(xlo.shape), whole(xlo.shape)]
    aliases = {2: 0}
    if with_image:
        in_specs += [whole(other.shape), whole(img.shape)]
        operands += [other, img]
        out_shape.append(jax.ShapeDtypeStruct(img.shape, jnp.float32))
        out_specs.append(whole(img.shape))
        aliases[8] = 3
    grid_spec = pltpu.PrefetchScalarGridSpec(
        num_scalar_prefetch=1,
        grid=(1,),
        in_specs=in_specs,
        out_specs=tuple(out_specs),
        scratch_shapes=[
            pltpu.VMEM((block_y + 2 * HALO, block_x, depth_z), jnp.float32),
            pltpu.VMEM((2, block_y, block_x, depth_z), jnp.float32),
        ],
    )
    return pl.pallas_call(
        functools.partial(wave_kernel, with_image),
        out_shape=tuple(out_shape),
        grid_spec=grid_spec,
        input_output_aliases=aliases,
        compiler_params=pltpu.CompilerParams(vmem_limit_bytes=48 * 1024 * 1024),
        cost_estimate=pl.CostEstimate(
            flops=60 * cur.size, bytes_accessed=4 * 6 * cur.size, transcendentals=0
        ),
    )(jnp.reshape(moment, (1,)).astype(jnp.int32), *operands)


def point_tables(cell_rows, x_start, cells_wide, depth_y):
    local_x = cell_rows[0] - x_start
    inside = (local_x >= 0) & (local_x < cells_wide)
    rows_y = (cell_rows[1][:, None] == jnp.arange(depth_y, dtype=jnp.int32)[None, :]).astype(
        jnp.float32
    )
    column = local_x * 4 + cell_rows[2]
    places = (column[:, None] == jnp.arange(cells_wide * 4, dtype=jnp.int32)[None, :]) & inside[
        :, None
    ]
    return (rows_y, places.astype(jnp.float32))


def spread_points(tables, amounts):
    rows_y, places = tables
    weighted = places[:, None, :] * jnp.transpose(amounts)[:, :, None]
    return jnp.einsum("ny,nsc->syc", rows_y, weighted, precision=lax.Precision.HIGHEST)


def shards(older_fields, fields_now, velocity, aperture, source_pos, wavelet, receiver_pos, traces):
    slab_count = lax.axis_size("dom")
    depth_y = fields_now.shape[1]
    cells_x = fields_now.shape[2]
    depth_z = fields_now.shape[3]
    block_y = velocity.shape[0]
    steps_total = wavelet.shape[0]
    x_anchor = lax.axis_index("dom") * cells_x
    bricks = velocity.reshape(block_y, slab_count, cells_x, depth_z)
    chosen = jnp.take(bricks, aperture, axis=1)
    arrived = lax.all_to_all(chosen, "dom", split_axis=1, concat_axis=0, tiled=True)
    scaled = courant * arrived.reshape(depth_y, cells_x, depth_z)
    speed_sq = scaled * scaled
    image_zero = jnp.zeros((depth_y, cells_x, depth_z), jnp.float32)
    source_core = point_tables(source_pos, x_anchor, cells_x, depth_y)
    receiver_core = point_tables(receiver_pos, x_anchor, cells_x, depth_y)

    planes = jnp.stack(
        [spread_points(source_core, wavelet), spread_points(receiver_core, traces)], axis=1
    )
    planes = planes.reshape(steps_total, 2, depth_y, cells_x, 4)
    gap = jnp.zeros((steps_total, 2, depth_y, depth_z - 4 * cells_x), jnp.float32)
    tail = planes[:, :, :, :0:-1].reshape(steps_total, 2, depth_y, 4 * (cells_x - 1))
    planes = jnp.concatenate([planes[:, :, :, 0], gap, tail], axis=3)
    planes = planes.reshape(steps_total, 2, depth_y, 1, depth_z)

    def advance(moment, state):
        (prev0, cur0, head0, tail0), (prev1, cur1, head1, tail1), image_acc = state
        low0, high0 = trade_halos(head0, tail0, "dom")
        low1, high1 = trade_halos(head1, tail1, "dom")
        new0, head0, tail0 = wave_call(0, moment, cur0, prev0, speed_sq, low0, high0, planes)
        new1, head1, tail1, image_acc = wave_call(
            1, moment, cur1, prev1, speed_sq, low1, high1, planes, new0, image_acc
        )
        return (cur0, new0, head0, tail0), (cur1, new1, head1, tail1), image_acc

    def pair(index, state):
        for offset in range(TRIP):
            state = advance(TRIP * index + offset, state)
        return state

    def edges(field):
        return (field[:, :HALO], field[:, cells_x - HALO :])

    start = (
        (older_fields[0], fields_now[0]) + edges(fields_now[0]),
        (older_fields[1], fields_now[1]) + edges(fields_now[1]),
        image_zero,
    )
    state = lax.fori_loop(0, steps_total // TRIP, pair, start)
    for moment in range(steps_total - steps_total % TRIP, steps_total):
        state = advance(moment, state)
    (prev0, cur0, _, _), (prev1, cur1, _, _), image_acc = state
    previous = jnp.stack([prev0, prev1])
    current = jnp.stack([cur0, cur1])
    image_acc = image_acc * (1.0 / steps_total)
    outgoing = image_acc.reshape(depth_y, 1, cells_x, depth_z)
    one_hot = (aperture[None, :] == jnp.arange(slab_count, dtype=jnp.int32)[:, None]).astype(
        jnp.float32
    )
    received = lax.all_to_all(outgoing, "dom", split_axis=0, concat_axis=1, tiled=True)
    summed = jnp.einsum("mj,yjcz->ymcz", one_hot, received, precision=lax.Precision.HIGHEST)
    image_model = summed.reshape(received.shape[0], slab_count * cells_x, received.shape[3])
    return (previous, current, image_model)


def solution(mesh):
    in_specs = (
        P(None, "survey", "dom", None),
        P(None, "survey", "dom", None),
        P("dom", "survey", None),
        P("survey"),
        P(None, "survey"),
        P(None, "survey"),
        P(None, "survey"),
        P(None, "survey"),
    )
    out_specs = (
        P(None, "survey", "dom", None),
        P(None, "survey", "dom", None),
        P("dom", "survey", None),
    )
    return jax.shard_map(shards, mesh=mesh, in_specs=in_specs, out_specs=out_specs, check_vma=False)
```
